128 devices in a mesh: grp: 4 (over y), dev: 32 (over z, x, core).
Axes of the slice: x: 4, y: 4, z: 4, core: 2. Of those that a mesh axis runs over, the one named last changes fastest.
Arguments:
- basis: float32 [8, 256, 16, 512], P(None, ('grp', 'dev')), may hold values from -6 to 6
- diagonal: float32 [256, 512], P(('grp', 'dev')), may hold values from 0.5 to 8
- near_blocks: bfloat16 [2048, 512, 512], P(('grp', 'dev')), may hold values from -0.03125 to 0.03125
- far_u: bfloat16 [14336, 32, 512], P(('grp', 'dev')), may hold values from -0.25 to 0.25
- far_v: bfloat16 [14336, 32, 512], P(('grp', 'dev')), may hold values from -0.125 to 0.125
- block_row: int32 [16384], P(('grp', 'dev')), may hold values from 0 to 1
- block_dest: int32 [16384, 1], P(('grp', 'dev')), may hold values from 0 to 127; in each aligned block of 128 rows (0 to 127, 128 to 255, ...) at most 2 rows name the same one
- block_col: int32 [16384], P(('grp', 'dev')), may hold values from 0 to 1
Outputs:
- next_vector: float32 [256, 16, 512], P(('grp', 'dev'))
- hess_column: float32 [9, 16], replicated
The draws below stay inside these ranges and needn't reach their ends.
Inputs may be any that keep to these rules, and one draw needn't show every extreme that they name: `block_dest`: among the 128 blocks of one device at most 2 name the same owning device, and this most is reached on some device.
All inputs are finite; a program needn't handle non-finite values.
Results may differ from the reference program's by a relative error of at most 0.0017.
Values sent between devices are 32-bit elements; how exact they have to be, the bound alone decides.
No kernel may reach another device: no remote copies, remote signals or barrier semaphores. Data moves between devices by JAX's collectives and lax.ppermute only.
A program may use at most 128 MiB of HBM per device.

```python
import math
import jax
import jax.numpy as jnp
import numpy as np
from jax import lax

CS = 512
RANK = 32
NRHS = 16
KRY = 8
CL_DEV = 2
NEAR_DEV = 16
FAR_DEV = 112
SLOTS_DEV = 128
CAP = 2
NC = 256
NEAR_ALL = 2048
FAR_ALL = 14336
SLOTS_ALL = 16384
N_GRP = 4
N_DEV = 32


def plant(entries, own_key, smallest, high):
    spot = [jax.random.randint(jax.random.fold_in(own_key, axis), (), 0, length) for axis, length in enumerate(entries.shape)]
    main_axis = entries.shape.index(max(entries.shape))
    beside = spot[:main_axis] + [(spot[main_axis] + 1) % entries.shape[main_axis]] + spot[main_axis + 1:]
    return entries.at[tuple(spot)].set(smallest).at[tuple(beside)].set(high)


def steps_of(key, dims, shards, smallest, top_value):
    def one(dim, shards_of):
        heights = jax.random.uniform(jax.random.fold_in(jax.random.fold_in(key, 6), dim), (shards_of,), jnp.float32, smallest / len(shards), top_value / len(shards))
        return jnp.repeat(jnp.exp(heights), dims[dim] // shards_of).reshape((-1,) + (1,) * (len(dims) - dim - 1))

    factor_of = one(*shards[0])
    for cut in shards[1:]:
        factor_of = factor_of * one(*cut)
    return factor_of


def routed_block(own_key, own, number, rows, number_of, top, limit, slope):
    ranking = jax.random.permutation(own_key, number_of)
    packed, usual = shares(number_of, rows * top, limit, slope, True), shares(number_of, rows * top, limit, slope, False)
    places = jnp.arange(number_of)

    def named(lengths, offset_by):
        used = int((lengths > 0).sum())
        fixed = max(1, used // 4)
        shifted = fixed + (places - fixed + offset_by * (used - fixed)) % max(1, number_of - fixed)
        return jnp.zeros((number_of,), jnp.int32).at[ranking[jnp.where(places < fixed, places, shifted)]].set(jnp.asarray(lengths, jnp.int32))

    lengths = jnp.where(number % 4 == 0, named(packed, number // 4), named(usual, number - number // 4 - 1))
    mixed = jax.random.permutation(jax.random.fold_in(own, 3), number_of)
    giver, taker = mixed[0:number_of // 2 * 2:2], mixed[1:number_of // 2 * 2:2]
    margin = jnp.minimum(lengths[giver] - 1, limit - lengths[taker]) // 2
    margin = jnp.where((giver == ranking[0]) | (taker == ranking[0]) | (lengths[taker] == 0), 0, jnp.maximum(margin, 0))
    shifted = jax.random.randint(jax.random.fold_in(own, 4), (number_of // 2,), 0, 1 << 20) % (margin + 1)
    lengths = lengths.at[giver].add(-shifted).at[taker].add(shifted)
    members = jnp.searchsorted(jnp.cumsum(lengths), jnp.arange(rows * top), side="right").astype(jnp.int32)
    listing = members.reshape(top, rows).T
    listing = listing[jax.random.permutation(jax.random.fold_in(own, 1), rows)]
    offset_by = jax.random.randint(jax.random.fold_in(own, 2), (rows, 1), 0, top)
    return jnp.take_along_axis(listing, (jnp.arange(top)[None, :] + offset_by) % top, axis=1)


def shares(amount, total, most, skew, full):
    portions = [(1 << 20) // math.isqrt(grade ** skew) + 1 for grade in range(1, amount + 1)]
    largest = most if full else min(most, max(-(-total // amount), total * portions[0] // sum(portions)))
    least = 1 if total - largest >= amount - 1 else 0
    given, surplus = [largest] + [least] * (amount - 1), total - largest - least * (amount - 1)
    while surplus > 0:
        candidates = [i for i in range(1, amount) if given[i] < largest] or [i for i in range(1, amount) if given[i] < most]
        whole, remaining = sum([portions[i] for i in candidates]), surplus
        for i in candidates:
            addition = min(most - given[i], max(1, remaining * portions[i] // whole), surplus)
            given[i] = given[i] + addition
            surplus = surplus - addition
    return np.array(given)


def bell_draw(key, dims, deviation, reach, cuts=(), kind=jnp.bfloat16):
    loudness = steps_of(key, dims, cuts, -0.22, 0.18) if cuts else 1.0
    entries = jax.random.normal(key, dims, jnp.float32) * deviation * loudness
    return jnp.minimum(jnp.maximum(entries, -reach), reach).astype(kind)


def setup_inputs(seed: int = 0) -> dict:
    keys = jax.random.split(jax.random.key(seed), 9)
    basis = bell_draw(keys[0], (KRY, NC, NRHS, CS), 1.0, 6.0, ((1, 128),), jnp.float32)
    diagonal = jnp.clip(jnp.exp(math.log(8.0) - 2.7725887 * jax.random.uniform(keys[1], (NC, CS), jnp.float32) ** steps_of(keys[1], (NC, CS), ((0, 128),), -0.2, 0.2)), 0.5, 8.0)
    near_blocks = bell_draw(keys[2], (NEAR_ALL, CS, CS), (CS * (NEAR_DEV + FAR_DEV) // CL_DEV) ** -0.5, 0.03125, ((0, 128),))
    far_u = bell_draw(keys[3], (FAR_ALL, RANK, CS), CS ** -0.5, 0.25, ((0, 128),))
    far_v = bell_draw(keys[4], (FAR_ALL, RANK, CS), (RANK * (NEAR_DEV + FAR_DEV) // CL_DEV) ** -0.5, 0.125, ((0, 128),))
    block_row = plant(jax.random.randint(keys[5], (SLOTS_ALL,), 0, CL_DEV), jax.random.fold_in(keys[5], 1), 0, CL_DEV - 1).astype(jnp.int32)
    block_dest_keys = jax.random.split(jax.random.fold_in(keys[6], 1), SLOTS_ALL // SLOTS_DEV)
    block_dest_turns = jax.random.permutation(jax.random.fold_in(keys[6], 3), SLOTS_ALL // SLOTS_DEV)
    block_dest = jax.vmap(lambda own, number: routed_block(jax.random.fold_in(keys[6], 2), own, number, SLOTS_DEV, N_GRP * N_DEV, 1, CAP, 2))(block_dest_keys, block_dest_turns).reshape((SLOTS_ALL, 1))
    block_col = plant(jax.random.randint(keys[7], (SLOTS_ALL,), 0, CL_DEV), jax.random.fold_in(keys[7], 1), 0, CL_DEV - 1).astype(jnp.int32)
    return dict(basis=basis, diagonal=diagonal, near_blocks=near_blocks, far_u=far_u, far_v=far_v, block_row=block_row, block_dest=block_dest, block_col=block_col)


def reference(basis, diagonal, near_blocks, far_u, far_v, block_row, block_dest, block_col):
    basis_count = basis.shape[0]
    clusters = basis.shape[1]
    devices = N_GRP * N_DEV
    slots = NEAR_DEV + FAR_DEV
    vector = basis[basis_count - 1]
    vec_low = vector.astype(jnp.bfloat16)
    target_dev = block_dest[:, 0].astype(jnp.int32)
    highest = lax.Precision.HIGHEST

    def per_device(total, device):
        start = (device * slots).astype(jnp.int32)
        rows = lax.dynamic_slice_in_dim(block_row, start, slots).astype(jnp.int32) + device * CL_DEV
        owners = lax.dynamic_slice_in_dim(target_dev, start, slots)
        columns = owners * CL_DEV + lax.dynamic_slice_in_dim(block_col, start, slots).astype(jnp.int32)
        near = lax.dynamic_slice_in_dim(near_blocks, (device * NEAR_DEV).astype(jnp.int32), NEAR_DEV).astype(jnp.float32)
        upper = lax.dynamic_slice_in_dim(far_u, (device * FAR_DEV).astype(jnp.int32), FAR_DEV).astype(jnp.float32)
        lower = lax.dynamic_slice_in_dim(far_v, (device * FAR_DEV).astype(jnp.int32), FAR_DEV).astype(jnp.float32)
        picked = vec_low[rows].astype(jnp.float32)
        near_part = jnp.einsum('snc,scd->snd', picked[:NEAR_DEV], near, precision=highest)
        coeff = jnp.einsum('snc,skc->snk', picked[NEAR_DEV:], upper, precision=highest).astype(jnp.bfloat16)
        coeff = lax.optimization_barrier(coeff).astype(jnp.float32)
        far_part = jnp.einsum('snk,skc->snc', coeff, lower, precision=highest)
        parts = jnp.concatenate([near_part, far_part], axis=0)
        return (total.at[columns].add(parts), None)
    start_total = jnp.zeros(vector.shape, jnp.float32)
    summed, unused = lax.scan(per_device, start_total, jnp.arange(devices, dtype=jnp.int32))
    image = diagonal[:, None, :] * vector + summed
    panels = clusters * CS
    first = jnp.einsum('knjc,njc->kj', basis, image, precision=highest) / panels
    once = image - jnp.einsum('kj,knjc->njc', first, basis, precision=highest)
    second = jnp.einsum('knjc,njc->kj', basis, once, precision=highest) / panels
    twice = once - jnp.einsum('kj,knjc->njc', second, basis, precision=highest)
    beta = jnp.sqrt(lax.optimization_barrier(jnp.sum(twice * twice, axis=(0, 2))) / panels + 1e-06)
    next_vector = twice / beta[None, :, None]
    hess_column = jnp.concatenate([first + second, beta[None, :]], axis=0)
    return (next_vector, hess_column)
```

```python
import jax
import jax.numpy as jnp
from jax import lax
from jax.sharding import PartitionSpec as P

AXES = ("grp", "dev")
SIZES = {"y": 4, "z": 4, "x": 4, "c": 2}
STRIDE = {"y": 32, "z": 8, "x": 2, "c": 1}


def coord(g, axis):
    return (g // STRIDE[axis]) % SIZES[axis]


def moved(axis, k):
    n, s = SIZES[axis], STRIDE[axis]
    pairs = []
    for g in range(128):
        c = (g // s) % n
        pairs.append((g, g + (((c + k) % n) - c) * s))
    return pairs


def flipped(bit):
    return [(g, g ^ (1 << bit)) for g in range(128)]


def all_sum(v):
    for bit in range(7):
        v = v + lax.ppermute(v, AXES, flipped(bit))
    return v


def reduce_to_owner(slab):
    rest = slab.shape[1:]
    slab = slab.reshape((2, -1) + rest[-2:])
    d = slab[0] + lax.ppermute(slab[1], AXES, moved("c", 1))
    for axis in ("x", "z", "y"):
        d = d.reshape((4, -1) + rest[-2:])
        acc = d[0]
        for k in (1, 2, 3):
            acc = acc + lax.ppermute(d[k], AXES, moved(axis, k))
        d = acc
    return d


def on_device(basis, diagonal, near_blocks, far_u, far_v, block_row, block_dest, block_col):
    highest = lax.Precision.HIGHEST
    basis_count = basis.shape[0]
    clusters = basis.shape[1]
    sources = basis.shape[2]
    cluster_size = basis.shape[3]
    near_count = near_blocks.shape[0]
    devices = lax.axis_size(AXES)
    me = lax.axis_index(AXES)
    vector = basis[basis_count - 1]
    vec_low = vector.astype(jnp.bfloat16)
    picked = vec_low[block_row]
    near_part = jnp.einsum(
        "snc,scd->snd", picked[:near_count], near_blocks, preferred_element_type=jnp.float32
    )
    coeff = jnp.einsum(
        "snc,skc->snk", picked[near_count:], far_u, preferred_element_type=jnp.float32
    ).astype(jnp.bfloat16)
    far_part = jnp.einsum("snk,skc->snc", coeff, far_v, preferred_element_type=jnp.float32)
    parts = jnp.concatenate([near_part, far_part], axis=0)
    dest = block_dest[:, 0]
    rel = {a: (coord(dest, a) - coord(me, a)) % SIZES[a] for a in SIZES}
    slot = (((rel["c"] * 4 + rel["x"]) * 4 + rel["z"]) * 4 + rel["y"]) * clusters + block_col
    slab = jnp.zeros((devices * clusters, sources, cluster_size), jnp.float32).at[slot].add(parts)
    summed = reduce_to_owner(slab.reshape(2, 4, 4, 4, clusters, sources, cluster_size))
    image = diagonal[:, None, :] * vector + summed
    panels = clusters * cluster_size * devices
    local_first = jnp.einsum("knjc,njc->kj", basis, image, precision=highest)
    local_gram = jnp.einsum("knjc,mnjc->kmj", basis, basis, precision=highest)
    both = all_sum(jnp.concatenate([local_first, local_gram.reshape(-1, sources)], axis=0))
    first = both[:basis_count] / panels
    gram = both[basis_count:].reshape(basis_count, basis_count, sources) / panels
    second = first - jnp.einsum("kmj,mj->kj", gram, first, precision=highest)
    total = first + second
    twice = image - jnp.einsum("kj,knjc->njc", total, basis, precision=highest)
    square = all_sum(jnp.sum(twice * twice, axis=(0, 2))) / panels
    beta = jnp.sqrt(square + 1e-06)
    next_vector = twice / beta[None, :, None]
    hess_column = jnp.concatenate([total, beta[None, :]], axis=0)
    return (next_vector, hess_column)


def solution(mesh):
    in_specs = (
        P(None, AXES, None, None),
        P(AXES, None),
        P(AXES, None, None),
        P(AXES, None, None),
        P(AXES, None, None),
        P(AXES),
        P(AXES, None),
        P(AXES),
    )
    out_specs = (P(AXES, None, None), P())
    return jax.shard_map(
        on_device, mesh=mesh, in_specs=in_specs, out_specs=out_specs, check_vma=False
    )
```

```python
import jax
import jax.numpy as jnp
from jax import lax
from jax.sharding import PartitionSpec as P

AXES = ("grp", "dev")
SIZES = {"y": 4, "z": 4, "x": 4, "c": 2}
STRIDE = {"y": 32, "z": 8, "x": 2, "c": 1}


def coord(g, axis):
    return (g // STRIDE[axis]) % SIZES[axis]


def moved(axis, k):
    n, s = SIZES[axis], STRIDE[axis]
    pairs = []
    for g in range(128):
        c = (g // s) % n
        pairs.append((g, g + (((c + k) % n) - c) * s))
    return pairs


def flipped(bit):
    return [(g, g ^ (1 << bit)) for g in range(128)]


def all_sum(v):
    for bit in range(7):
        v = v + lax.ppermute(v, AXES, flipped(bit))
    return v


def spread(pieces, axis):
    acc = pieces[0]
    for k in (1, 2, 3):
        acc = acc + lax.ppermute(pieces[k], AXES, moved(axis, k))
    return acc


def reduce_to_owner(keep, send):
    tail = keep.shape[1:]
    d = keep + lax.ppermute(send, AXES, moved("c", 1))
    first_half = d[:64].reshape((4, 16) + tail)
    second_half = d[64:].reshape((4, 16) + tail)
    a = spread(first_half, "x").reshape((4, 4) + tail)
    b = spread(second_half, "z").reshape((4, 4) + tail)
    a = spread(a, "z")
    b = spread(b, "x")
    return spread(jnp.stack([a, b], axis=1), "y")


def on_device(basis, diagonal, near_blocks, far_u, far_v, block_row, block_dest, block_col):
    highest = lax.Precision.HIGHEST
    basis_count = basis.shape[0]
    clusters = basis.shape[1]
    sources = basis.shape[2]
    cluster_size = basis.shape[3]
    near_count = near_blocks.shape[0]
    devices = lax.axis_size(AXES)
    me = lax.axis_index(AXES)
    vector = basis[basis_count - 1]
    vec_low = vector.astype(jnp.bfloat16)
    picked = vec_low[block_row]
    near_part = jnp.einsum(
        "snc,scd->snd", picked[:near_count], near_blocks, preferred_element_type=jnp.float32
    )
    coeff = jnp.einsum(
        "snc,skc->snk", picked[near_count:], far_u, preferred_element_type=jnp.float32
    ).astype(jnp.bfloat16)
    far_part = jnp.einsum("snk,skc->snc", coeff, far_v, preferred_element_type=jnp.float32)
    dest = block_dest[:, 0]
    rel = {a: (coord(dest, a) - coord(me, a)) % SIZES[a] for a in SIZES}
    inner = jnp.where(
        block_col == 0,
        (rel["x"] * 4 + rel["z"]) * 4 + rel["y"],
        64 + (rel["z"] * 4 + rel["x"]) * 4 + rel["y"],
    )
    slot = rel["c"] * 128 + inner
    rows = jnp.arange(128, dtype=slot.dtype)[:, None]
    flat_near = near_part.reshape(near_count, -1)
    flat_far = far_part.reshape(far_part.shape[0], -1)

    def gathered(offset):
        hits = (slot[None, :] == rows + offset).astype(jnp.float32)
        out = jnp.dot(hits[:, :near_count], flat_near, precision=highest)
        out = out + jnp.dot(hits[:, near_count:], flat_far, precision=highest)
        return out.reshape(128, sources, cluster_size)

    summed = reduce_to_owner(gathered(0), gathered(128))
    image = diagonal[:, None, :] * vector + summed
    panels = clusters * cluster_size * devices
    local_first = jnp.einsum("knjc,njc->kj", basis, image, precision=highest)
    local_gram = jnp.einsum("knjc,mnjc->kmj", basis, basis, precision=highest)
    both = all_sum(jnp.concatenate([local_first, local_gram.reshape(-1, sources)], axis=0))
    first = both[:basis_count] / panels
    gram = both[basis_count:].reshape(basis_count, basis_count, sources) / panels
    second = first - jnp.einsum("kmj,mj->kj", gram, first, precision=highest)
    total = first + second
    twice = image - jnp.einsum("kj,knjc->njc", total, basis, precision=highest)
    square = all_sum(jnp.sum(twice * twice, axis=(0, 2))) / panels
    beta = jnp.sqrt(square + 1e-06)
    next_vector = twice / beta[None, :, None]
    hess_column = jnp.concatenate([total, beta[None, :]], axis=0)
    return (next_vector, hess_column)


def solution(mesh):
    in_specs = (
        P(None, AXES, None, None),
        P(AXES, None),
        P(AXES, None, None),
        P(AXES, None, None),
        P(AXES, None, None),
        P(AXES),
        P(AXES, None),
        P(AXES),
    )
    out_specs = (P(AXES, None, None), P())
    return jax.shard_map(
        on_device, mesh=mesh, in_specs=in_specs, out_specs=out_specs, check_vma=False
    )
```

```python
import jax
import jax.numpy as jnp
from jax import lax
from jax.sharding import PartitionSpec as P

AXES = ("grp", "dev")
SIZES = {"y": 4, "z": 4, "x": 4, "c": 2}
STRIDE = {"y": 32, "z": 8, "x": 2, "c": 1}


def coord(g, axis):
    return (g // STRIDE[axis]) % SIZES[axis]


def moved(axis, k, other=None):
    pairs = []
    for g in range(128):
        a = other if (other is not None and g % 2 == 1) else axis
        n, s = SIZES[a], STRIDE[a]
        c = (g // s) % n
        pairs.append((g, g + (((c + k) % n) - c) * s))
    return pairs


def flipped(bit):
    return [(g, g ^ (1 << bit)) for g in range(128)]


def all_sum(v):
    for bit in range(7):
        v = v + lax.ppermute(v, AXES, flipped(bit))
    return v


def spread(pieces, axis, other=None):
    acc = pieces[0]
    for k in (1, 2, 3):
        acc = acc + lax.ppermute(pieces[k], AXES, moved(axis, k, other))
    return acc


def reduce_to_owner(keep, send):
    d = keep + lax.ppermute(send, AXES, moved("c", 1))
    d = spread(d, "x", "z")
    d = spread(d, "z", "x")
    return spread(d, "y")


def on_device(basis, diagonal, near_blocks, far_u, far_v, block_row, block_dest, block_col):
    highest = lax.Precision.HIGHEST
    basis_count = basis.shape[0]
    clusters = basis.shape[1]
    sources = basis.shape[2]
    cluster_size = basis.shape[3]
    near_count = near_blocks.shape[0]
    devices = lax.axis_size(AXES)
    me = lax.axis_index(AXES)
    vector = basis[basis_count - 1]
    vec_low = vector.astype(jnp.bfloat16)
    picked = vec_low[block_row]
    near_part = jnp.einsum(
        "snc,scd->snd", picked[:near_count], near_blocks, preferred_element_type=jnp.float32
    )
    coeff = jnp.einsum(
        "snc,skc->snk", picked[near_count:], far_u, preferred_element_type=jnp.float32
    ).astype(jnp.bfloat16)
    far_part = jnp.einsum("snk,skc->snc", coeff, far_v, preferred_element_type=jnp.float32)
    dest = block_dest[:, 0]
    rel = {a: (coord(dest, a) - coord(me, a)) % SIZES[a] for a in SIZES}
    to_core = coord(dest, "c")
    order = jnp.where(to_core == 0, rel["x"] * 4 + rel["z"], rel["z"] * 4 + rel["x"])
    slot = ((rel["c"] * 16 + order) * 4 + rel["y"]) * clusters + block_col
    blocks = slot.shape[0]
    numbers = jnp.arange(blocks, dtype=jnp.int32)
    spots = devices * clusters
    lowest = jnp.full((spots,), blocks, jnp.int32).at[slot].min(numbers)
    highest_block = jnp.full((spots,), -1, jnp.int32).at[slot].max(numbers)
    second_block = jnp.where(highest_block > lowest, highest_block, blocks)
    table = jnp.concatenate(
        [near_part, far_part, jnp.zeros((1, sources, cluster_size), jnp.float32)], axis=0
    )
    slab = table[lowest] + table[second_block]
    shape = (2, 4, 4, 4, clusters, sources, cluster_size)
    slab = slab.reshape(shape)
    summed = reduce_to_owner(slab[0], slab[1])
    image = diagonal[:, None, :] * vector + summed
    panels = clusters * cluster_size * devices
    local_first = jnp.einsum("knjc,njc->kj", basis, image, precision=highest)
    local_gram = jnp.einsum("knjc,mnjc->kmj", basis, basis, precision=highest)
    both = all_sum(jnp.concatenate([local_first, local_gram.reshape(-1, sources)], axis=0))
    first = both[:basis_count] / panels
    gram = both[basis_count:].reshape(basis_count, basis_count, sources) / panels
    second = first - jnp.einsum("kmj,mj->kj", gram, first, precision=highest)
    total = first + second
    twice = image - jnp.einsum("kj,knjc->njc", total, basis, precision=highest)
    square = all_sum(jnp.sum(twice * twice, axis=(0, 2))) / panels
    beta = jnp.sqrt(square + 1e-06)
    next_vector = twice / beta[None, :, None]
    hess_column = jnp.concatenate([total, beta[None, :]], axis=0)
    return (next_vector, hess_column)


def solution(mesh):
    in_specs = (
        P(None, AXES, None, None),
        P(AXES, None),
        P(AXES, None, None),
        P(AXES, None, None),
        P(AXES, None, None),
        P(AXES),
        P(AXES, None),
        P(AXES),
    )
    out_specs = (P(AXES, None, None), P())
    return jax.shard_map(
        on_device, mesh=mesh, in_specs=in_specs, out_specs=out_specs, check_vma=False
    )
```

```python
import jax
import jax.numpy as jnp
from jax import lax
from jax.experimental import pallas as pl
from jax.experimental.pallas import tpu as pltpu
from jax.sharding import PartitionSpec as P

AXES = ("grp", "dev")
SIZES = {"y": 4, "z": 4, "x": 4, "c": 2}
STRIDE = {"y": 32, "z": 8, "x": 2, "c": 1}


def coord(g, axis):
    return (g // STRIDE[axis]) % SIZES[axis]


def moved(axis, k, other=None):
    pairs = []
    for g in range(128):
        a = other if (other is not None and g % 2 == 1) else axis
        n, s = SIZES[a], STRIDE[a]
        c = (g // s) % n
        pairs.append((g, g + (((c + k) % n) - c) * s))
    return pairs


def flipped(bit):
    return [(g, g ^ (1 << bit)) for g in range(128)]


def all_sum(v):
    for bit in range(7):
        v = v + lax.ppermute(v, AXES, flipped(bit))
    return v


def spread(pieces, axis, other=None):
    acc = pieces[0]
    for k in (1, 2, 3):
        acc = acc + lax.ppermute(pieces[k], AXES, moved(axis, k, other))
    return acc


def reduce_to_owner(keep, send):
    d = keep + lax.ppermute(send, AXES, moved("c", 1))
    d = spread(d, "x", "z")
    d = spread(d, "z", "x")
    return spread(d, "y")


STEPS = 8

def block_kernel(slot_ref, row_ref, vec_ref, near_ref, u_ref, v_ref, keep_ref, send_ref):
    i = pl.program_id(0)
    half = keep_ref.shape[0]
    near_step = near_ref.shape[0]
    far_step = u_ref.shape[0]
    near_total = near_step * pl.num_programs(0)

    @pl.when(i == 0)
    def _():
        keep_ref[...] = jnp.zeros_like(keep_ref)
        send_ref[...] = jnp.zeros_like(send_ref)

    def add(g, part):
        s = slot_ref[g]

        @pl.when(s < half)
        def _():
            keep_ref[s] += part

        @pl.when(s >= half)
        def _():
            send_ref[s - half] += part

    for j in range(near_step):
        g = i * near_step + j
        a = vec_ref[row_ref[g]]
        add(g, jnp.dot(a, near_ref[j], preferred_element_type=jnp.float32))
    for j in range(far_step):
        g = near_total + i * far_step + j
        a = vec_ref[row_ref[g]]
        coeff = lax.dot_general(a, u_ref[j], (((1,), (1,)), ((), ())), preferred_element_type=jnp.float32)
        add(g, jnp.dot(coeff.astype(jnp.bfloat16), v_ref[j], preferred_element_type=jnp.float32))


def block_products(slot, rows, vec_low, near_blocks, far_u, far_v, half):
    near_count, size, _ = near_blocks.shape
    far_count, rank, _ = far_u.shape
    sources = vec_low.shape[1]
    near_step = near_count // STEPS
    far_step = far_count // STEPS
    out = jax.ShapeDtypeStruct((half, sources, size), jnp.float32)
    grid_spec = pltpu.PrefetchScalarGridSpec(
        num_scalar_prefetch=2,
        grid=(STEPS,),
        in_specs=[
            pl.BlockSpec(vec_low.shape, lambda i, s, r: (0, 0, 0)),
            pl.BlockSpec((near_step, size, size), lambda i, s, r: (i, 0, 0)),
            pl.BlockSpec((far_step, rank, size), lambda i, s, r: (i, 0, 0)),
            pl.BlockSpec((far_step, rank, size), lambda i, s, r: (i, 0, 0)),
        ],
        out_specs=[
            pl.BlockSpec((half, sources, size), lambda i, s, r: (0, 0, 0)),
            pl.BlockSpec((half, sources, size), lambda i, s, r: (0, 0, 0)),
        ],
    )
    return pl.pallas_call(
        block_kernel,
        grid_spec=grid_spec,
        out_shape=[out, out],
        compiler_params=pltpu.CompilerParams(
            dimension_semantics=("arbitrary",), vmem_limit_bytes=48 * 1024 * 1024
        ),
    )(slot, rows, vec_low, near_blocks, far_u, far_v)


def on_device(basis, diagonal, near_blocks, far_u, far_v, block_row, block_dest, block_col):
    highest = lax.Precision.HIGHEST
    basis_count = basis.shape[0]
    clusters = basis.shape[1]
    sources = basis.shape[2]
    cluster_size = basis.shape[3]
    near_count = near_blocks.shape[0]
    devices = lax.axis_size(AXES)
    me = lax.axis_index(AXES)
    vector = basis[basis_count - 1]
    vec_low = vector.astype(jnp.bfloat16)
    dest = block_dest[:, 0]
    rel = {a: (coord(dest, a) - coord(me, a)) % SIZES[a] for a in SIZES}
    to_core = coord(dest, "c")
    order = jnp.where(to_core == 0, rel["x"] * 4 + rel["z"], rel["z"] * 4 + rel["x"])
    slot = ((rel["c"] * 16 + order) * 4 + rel["y"]) * clusters + block_col
    spots = devices * clusters
    keep, send = block_products(slot, block_row, vec_low, near_blocks, far_u, far_v, spots // 2)
    shape = (4, 4, 4, clusters, sources, cluster_size)
    summed = reduce_to_owner(keep.reshape(shape), send.reshape(shape))
    image = diagonal[:, None, :] * vector + summed
    panels = clusters * cluster_size * devices
    local_first = jnp.einsum("knjc,njc->kj", basis, image, precision=highest)
    local_gram = jnp.einsum("knjc,mnjc->kmj", basis, basis, precision=highest)
    both = all_sum(jnp.concatenate([local_first, local_gram.reshape(-1, sources)], axis=0))
    first = both[:basis_count] / panels
    gram = both[basis_count:].reshape(basis_count, basis_count, sources) / panels
    second = first - jnp.einsum("kmj,mj->kj", gram, first, precision=highest)
    total = first + second
    twice = image - jnp.einsum("kj,knjc->njc", total, basis, precision=highest)
    square = all_sum(jnp.sum(twice * twice, axis=(0, 2))) / panels
    beta = jnp.sqrt(square + 1e-06)
    next_vector = twice / beta[None, :, None]
    hess_column = jnp.concatenate([total, beta[None, :]], axis=0)
    return (next_vector, hess_column)


def solution(mesh):
    in_specs = (
        P(None, AXES, None, None),
        P(AXES, None),
        P(AXES, None, None),
        P(AXES, None, None),
        P(AXES, None, None),
        P(AXES),
        P(AXES, None),
        P(AXES),
    )
    out_specs = (P(AXES, None, None), P())
    return jax.shard_map(
        on_device, mesh=mesh, in_specs=in_specs, out_specs=out_specs, check_vma=False
    )
```

```python
import jax
import jax.numpy as jnp
from jax import lax
from jax.experimental import pallas as pl
from jax.experimental.pallas import tpu as pltpu
from jax.sharding import PartitionSpec as P

AXES = ("grp", "dev")
SIZES = {"y": 4, "z": 4, "x": 4, "c": 2}
STRIDE = {"y": 32, "z": 8, "x": 2, "c": 1}


def coord(g, axis):
    return (g // STRIDE[axis]) % SIZES[axis]


def moved(axis, k, other=None):
    pairs = []
    for g in range(128):
        a = other if (other is not None and g % 2 == 1) else axis
        n, s = SIZES[a], STRIDE[a]
        c = (g // s) % n
        pairs.append((g, g + (((c + k) % n) - c) * s))
    return pairs


def flipped(bit):
    return [(g, g ^ (1 << bit)) for g in range(128)]


def all_sum(v):
    for bit in range(7):
        v = v + lax.ppermute(v, AXES, flipped(bit))
    return v


def spread(pieces, axis, other=None):
    acc = pieces[0]
    for k in (1, 2, 3):
        acc = acc + lax.ppermute(pieces[k], AXES, moved(axis, k, other))
    return acc


def reduce_to_owner(keep, send):
    d = keep + lax.ppermute(send, AXES, moved("c", 1))
    d = spread(d, "x", "z")
    d = spread(d, "z", "x")
    return spread(d, "y")


STEPS = 8


def accumulate_kernel(slot_ref, near_ref, far_ref, keep_ref, send_ref):
    i = pl.program_id(0)
    half = keep_ref.shape[0]
    near_step = near_ref.shape[0]
    far_step = far_ref.shape[0]
    near_total = near_step * pl.num_programs(0)

    @pl.when(i == 0)
    def _():
        keep_ref[...] = jnp.zeros_like(keep_ref)
        send_ref[...] = jnp.zeros_like(send_ref)

    def add(g, part):
        s = slot_ref[g]

        @pl.when(s < half)
        def _():
            keep_ref[s] += part

        @pl.when(s >= half)
        def _():
            send_ref[s - half] += part

    for j in range(near_step):
        add(i * near_step + j, near_ref[j])
    for j in range(far_step):
        add(near_total + i * far_step + j, far_ref[j])


def accumulate(slot, near_part, far_part, half):
    near_count, sources, size = near_part.shape
    far_count = far_part.shape[0]
    near_step = near_count // STEPS
    far_step = far_count // STEPS
    out = jax.ShapeDtypeStruct((half, sources, size), jnp.float32)
    grid_spec = pltpu.PrefetchScalarGridSpec(
        num_scalar_prefetch=1,
        grid=(STEPS,),
        in_specs=[
            pl.BlockSpec((near_step, sources, size), lambda i, s: (i, 0, 0)),
            pl.BlockSpec((far_step, sources, size), lambda i, s: (i, 0, 0)),
        ],
        out_specs=[
            pl.BlockSpec((half, sources, size), lambda i, s: (0, 0, 0)),
            pl.BlockSpec((half, sources, size), lambda i, s: (0, 0, 0)),
        ],
    )
    return pl.pallas_call(
        accumulate_kernel,
        grid_spec=grid_spec,
        out_shape=[out, out],
        compiler_params=pltpu.CompilerParams(
            dimension_semantics=("arbitrary",), vmem_limit_bytes=48 * 1024 * 1024
        ),
    )(slot, near_part, far_part)


def on_device(basis, diagonal, near_blocks, far_u, far_v, block_row, block_dest, block_col):
    highest = lax.Precision.HIGHEST
    basis_count = basis.shape[0]
    clusters = basis.shape[1]
    sources = basis.shape[2]
    cluster_size = basis.shape[3]
    near_count = near_blocks.shape[0]
    devices = lax.axis_size(AXES)
    me = lax.axis_index(AXES)
    vector = basis[basis_count - 1]
    vec_low = vector.astype(jnp.bfloat16)
    picked = vec_low[block_row]
    near_part = jnp.einsum(
        "snc,scd->snd", picked[:near_count], near_blocks, preferred_element_type=jnp.float32
    )
    coeff = jnp.einsum(
        "snc,skc->snk", picked[near_count:], far_u, preferred_element_type=jnp.float32
    ).astype(jnp.bfloat16)
    far_part = jnp.einsum("snk,skc->snc", coeff, far_v, preferred_element_type=jnp.float32)
    dest = block_dest[:, 0]
    rel = {a: (coord(dest, a) - coord(me, a)) % SIZES[a] for a in SIZES}
    to_core = coord(dest, "c")
    order = jnp.where(to_core == 0, rel["x"] * 4 + rel["z"], rel["z"] * 4 + rel["x"])
    slot = ((rel["c"] * 16 + order) * 4 + rel["y"]) * clusters + block_col
    spots = devices * clusters
    keep, send = accumulate(slot, near_part, far_part, spots // 2)
    shape = (4, 4, 4, clusters, sources, cluster_size)
    summed = reduce_to_owner(keep.reshape(shape), send.reshape(shape))
    image = diagonal[:, None, :] * vector + summed
    panels = clusters * cluster_size * devices
    local_first = jnp.einsum("knjc,njc->kj", basis, image, precision=highest)
    local_gram = jnp.einsum("knjc,mnjc->kmj", basis, basis, precision=highest)
    both = all_sum(jnp.concatenate([local_first, local_gram.reshape(-1, sources)], axis=0))
    first = both[:basis_count] / panels
    gram = both[basis_count:].reshape(basis_count, basis_count, sources) / panels
    second = first - jnp.einsum("kmj,mj->kj", gram, first, precision=highest)
    total = first + second
    twice = image - jnp.einsum("kj,knjc->njc", total, basis, precision=highest)
    square = all_sum(jnp.sum(twice * twice, axis=(0, 2))) / panels
    beta = jnp.sqrt(square + 1e-06)
    next_vector = twice / beta[None, :, None]
    hess_column = jnp.concatenate([total, beta[None, :]], axis=0)
    return (next_vector, hess_column)


def solution(mesh):
    in_specs = (
        P(None, AXES, None, None),
        P(AXES, None),
        P(AXES, None, None),
        P(AXES, None, None),
        P(AXES, None, None),
        P(AXES),
        P(AXES, None),
        P(AXES),
    )
    out_specs = (P(AXES, None, None), P())
    return jax.shard_map(
        on_device, mesh=mesh, in_specs=in_specs, out_specs=out_specs, check_vma=False
    )
```

```python
import jax
import jax.numpy as jnp
from jax import lax
from jax.experimental import pallas as pl
from jax.experimental.pallas import tpu as pltpu
from jax.sharding import PartitionSpec as P

AXES = ("grp", "dev")
SIZES = {"y": 4, "z": 4, "x": 4, "c": 2}
STRIDE = {"y": 32, "z": 8, "x": 2, "c": 1}


def coord(g, axis):
    return (g // STRIDE[axis]) % SIZES[axis]


def moved(axis, k, other=None):
    pairs = []
    for g in range(128):
        a = other if (other is not None and g % 2 == 1) else axis
        n, s = SIZES[a], STRIDE[a]
        c = (g // s) % n
        pairs.append((g, g + (((c + k) % n) - c) * s))
    return pairs


def flipped(mask):
    return [(g, g ^ mask) for g in range(128)]


def all_sum(v):
    v = v + lax.ppermute(v, AXES, flipped(1))
    for axis in ("x", "z", "y"):
        for step in (1, 3):
            v = v + lax.ppermute(v, AXES, flipped(step * STRIDE[axis]))
    return v


def spread(pieces, axis, other=None):
    acc = pieces[0]
    for k in (1, 2, 3):
        acc = acc + lax.ppermute(pieces[k], AXES, moved(axis, k, other))
    return acc


def reduce_to_owner(keep, send):
    pieces = [keep[k] + lax.ppermute(send[k], AXES, moved("c", 1)) for k in range(4)]
    acc = pieces[0]
    for k in (1, 2, 3):
        acc = acc + lax.ppermute(pieces[k], AXES, moved("x", k, "z"))
    d = spread(acc, "z", "x")
    return spread(d, "y")


STEPS = 8


def accumulate_kernel(slot_ref, near_ref, far_ref, keep_ref, send_ref):
    i = pl.program_id(0)
    half = keep_ref.shape[0]
    near_step = near_ref.shape[0]
    far_step = far_ref.shape[0]
    near_total = near_step * pl.num_programs(0)

    @pl.when(i == 0)
    def _():
        keep_ref[...] = jnp.zeros_like(keep_ref)
        send_ref[...] = jnp.zeros_like(send_ref)

    def add(g, part):
        s = slot_ref[g]

        @pl.when(s < half)
        def _():
            keep_ref[s] += part

        @pl.when(s >= half)
        def _():
            send_ref[s - half] += part

    for j in range(near_step):
        add(i * near_step + j, near_ref[j])
    for j in range(far_step):
        add(near_total + i * far_step + j, far_ref[j])


def accumulate(slot, near_part, far_part, half):
    near_count, sources, size = near_part.shape
    far_count = far_part.shape[0]
    near_step = near_count // STEPS
    far_step = far_count // STEPS
    out = jax.ShapeDtypeStruct((half, sources, size), jnp.float32)
    grid_spec = pltpu.PrefetchScalarGridSpec(
        num_scalar_prefetch=1,
        grid=(STEPS,),
        in_specs=[
            pl.BlockSpec((near_step, sources, size), lambda i, s: (i, 0, 0)),
            pl.BlockSpec((far_step, sources, size), lambda i, s: (i, 0, 0)),
        ],
        out_specs=[
            pl.BlockSpec((half, sources, size), lambda i, s: (0, 0, 0)),
            pl.BlockSpec((half, sources, size), lambda i, s: (0, 0, 0)),
        ],
    )
    return pl.pallas_call(
        accumulate_kernel,
        grid_spec=grid_spec,
        out_shape=[out, out],
        compiler_params=pltpu.CompilerParams(
            dimension_semantics=("arbitrary",), vmem_limit_bytes=48 * 1024 * 1024
        ),
    )(slot, near_part, far_part)


def on_device(basis, diagonal, near_blocks, far_u, far_v, block_row, block_dest, block_col):
    highest = lax.Precision.HIGHEST
    basis_count = basis.shape[0]
    clusters = basis.shape[1]
    sources = basis.shape[2]
    cluster_size = basis.shape[3]
    near_count = near_blocks.shape[0]
    devices = lax.axis_size(AXES)
    me = lax.axis_index(AXES)
    vector = basis[basis_count - 1]
    vec_low = vector.astype(jnp.bfloat16)
    picked = vec_low[block_row]
    near_part = jnp.einsum(
        "snc,scd->snd", picked[:near_count], near_blocks, preferred_element_type=jnp.float32
    )
    coeff = jnp.einsum(
        "snc,skc->snk", picked[near_count:], far_u, preferred_element_type=jnp.float32
    ).astype(jnp.bfloat16)
    far_part = jnp.einsum("snk,skc->snc", coeff, far_v, preferred_element_type=jnp.float32)
    dest = block_dest[:, 0]
    rel = {a: (coord(dest, a) - coord(me, a)) % SIZES[a] for a in SIZES}
    to_core = coord(dest, "c")
    order = jnp.where(to_core == 0, rel["x"] * 4 + rel["z"], rel["z"] * 4 + rel["x"])
    slot = ((rel["c"] * 16 + order) * 4 + rel["y"]) * clusters + block_col
    spots = devices * clusters
    keep, send = accumulate(slot, near_part, far_part, spots // 2)
    shape = (4, 4, 4, clusters, sources, cluster_size)
    summed = reduce_to_owner(keep.reshape(shape), send.reshape(shape))
    image = diagonal[:, None, :] * vector + summed
    panels = clusters * cluster_size * devices
    local_first = jnp.einsum("knjc,njc->kj", basis, image, precision=highest)
    local_gram = jnp.einsum("knjc,mnjc->kmj", basis, basis, precision=highest)
    both = all_sum(jnp.concatenate([local_first, local_gram.reshape(-1, sources)], axis=0))
    first = both[:basis_count] / panels
    gram = both[basis_count:].reshape(basis_count, basis_count, sources) / panels
    second = first - jnp.einsum("kmj,mj->kj", gram, first, precision=highest)
    total = first + second
    twice = image - jnp.einsum("kj,knjc->njc", total, basis, precision=highest)
    square = all_sum(jnp.sum(twice * twice, axis=(0, 2))) / panels
    beta = jnp.sqrt(square + 1e-06)
    next_vector = twice / beta[None, :, None]
    hess_column = jnp.concatenate([total, beta[None, :]], axis=0)
    return (next_vector, hess_column)


def solution(mesh):
    in_specs = (
        P(None, AXES, None, None),
        P(AXES, None),
        P(AXES, None, None),
        P(AXES, None, None),
        P(AXES, None, None),
        P(AXES),
        P(AXES, None),
        P(AXES),
    )
    out_specs = (P(AXES, None, None), P())
    return jax.shard_map(
        on_device, mesh=mesh, in_specs=in_specs, out_specs=out_specs, check_vma=False
    )
```

```python
import jax
import jax.numpy as jnp
from jax import lax
from jax.experimental import pallas as pl
from jax.experimental.pallas import tpu as pltpu
from jax.sharding import PartitionSpec as P

AXES = ("grp", "dev")
SIZES = {"y": 4, "z": 4, "x": 4, "c": 2}
STRIDE = {"y": 32, "z": 8, "x": 2, "c": 1}


def coord(g, axis):
    return (g // STRIDE[axis]) % SIZES[axis]


def moved(axis, k, other=None):
    pairs = []
    for g in range(128):
        a = other if (other is not None and g % 2 == 1) else axis
        n, s = SIZES[a], STRIDE[a]
        c = (g // s) % n
        pairs.append((g, g + (((c + k) % n) - c) * s))
    return pairs


def flipped(mask):
    return [(g, g ^ mask) for g in range(128)]


def all_sum(v):
    v = v + lax.ppermute(v, AXES, flipped(1))
    for axis in ("x", "z", "y"):
        for step in (1, 3):
            v = v + lax.ppermute(v, AXES, flipped(step * STRIDE[axis]))
    return v


def spread(pieces, axis, other=None):
    acc = pieces[0]
    for k in (1, 2, 3):
        acc = acc + lax.ppermute(pieces[k], AXES, moved(axis, k, other))
    return acc


def reduce_to_owner(keep, send):
    pieces = [keep[k] + lax.ppermute(send[k], AXES, moved("c", 1)) for k in range(4)]
    acc = pieces[0]
    for k in (1, 2, 3):
        acc = acc + lax.ppermute(pieces[k], AXES, moved("x", k, "z"))
    d = spread(acc, "z", "x")
    return spread(d, "y")


STEPS = 8


def accumulate_kernel(slot_ref, near_ref, far_ref, *out_refs):
    i = pl.program_id(0)
    piece = out_refs[0].shape[0]
    near_step = near_ref.shape[0]
    far_step = far_ref.shape[0]
    near_total = near_step * pl.num_programs(0)

    @pl.when(i == 0)
    def _():
        for ref in out_refs:
            ref[...] = jnp.zeros_like(ref)

    def add(g, part):
        s = slot_ref[g]
        for number, ref in enumerate(out_refs):

            @pl.when(s // piece == number)
            def _():
                ref[s % piece] += part

    for j in range(near_step):
        add(i * near_step + j, near_ref[j])
    for j in range(far_step):
        add(near_total + i * far_step + j, far_ref[j])


def accumulate(slot, near_part, far_part, spots, pieces):
    near_count, sources, size = near_part.shape
    far_count = far_part.shape[0]
    near_step = near_count // STEPS
    far_step = far_count // STEPS
    length = spots // pieces
    out = jax.ShapeDtypeStruct((length, sources, size), jnp.float32)
    grid_spec = pltpu.PrefetchScalarGridSpec(
        num_scalar_prefetch=1,
        grid=(STEPS,),
        in_specs=[
            pl.BlockSpec((near_step, sources, size), lambda i, s: (i, 0, 0)),
            pl.BlockSpec((far_step, sources, size), lambda i, s: (i, 0, 0)),
        ],
        out_specs=[pl.BlockSpec((length, sources, size), lambda i, s: (0, 0, 0))] * pieces,
    )
    return pl.pallas_call(
        accumulate_kernel,
        grid_spec=grid_spec,
        out_shape=[out] * pieces,
        compiler_params=pltpu.CompilerParams(
            dimension_semantics=("arbitrary",), vmem_limit_bytes=48 * 1024 * 1024
        ),
    )(slot, near_part, far_part)


def on_device(basis, diagonal, near_blocks, far_u, far_v, block_row, block_dest, block_col):
    highest = lax.Precision.HIGHEST
    basis_count = basis.shape[0]
    clusters = basis.shape[1]
    sources = basis.shape[2]
    cluster_size = basis.shape[3]
    near_count = near_blocks.shape[0]
    devices = lax.axis_size(AXES)
    me = lax.axis_index(AXES)
    vector = basis[basis_count - 1]
    vec_low = vector.astype(jnp.bfloat16)
    picked = vec_low[block_row]
    near_part = jnp.einsum(
        "snc,scd->snd", picked[:near_count], near_blocks, preferred_element_type=jnp.float32
    )
    coeff = jnp.einsum(
        "snc,skc->snk", picked[near_count:], far_u, preferred_element_type=jnp.float32
    ).astype(jnp.bfloat16)
    far_part = jnp.einsum("snk,skc->snc", coeff, far_v, preferred_element_type=jnp.float32)
    dest = block_dest[:, 0]
    rel = {a: (coord(dest, a) - coord(me, a)) % SIZES[a] for a in SIZES}
    to_core = coord(dest, "c")
    order = jnp.where(to_core == 0, rel["x"] * 4 + rel["z"], rel["z"] * 4 + rel["x"])
    slot = ((rel["c"] * 16 + order) * 4 + rel["y"]) * clusters + block_col
    spots = devices * clusters
    parts = accumulate(slot, near_part, far_part, spots, 8)
    shape = (4, 4, clusters, sources, cluster_size)
    parts = [p.reshape(shape) for p in parts]
    summed = reduce_to_owner(parts[:4], parts[4:])
    image = diagonal[:, None, :] * vector + summed
    panels = clusters * cluster_size * devices
    local_first = jnp.einsum("knjc,njc->kj", basis, image, precision=highest)
    local_gram = jnp.einsum("knjc,mnjc->kmj", basis, basis, precision=highest)
    both = all_sum(jnp.concatenate([local_first, local_gram.reshape(-1, sources)], axis=0))
    first = both[:basis_count] / panels
    gram = both[basis_count:].reshape(basis_count, basis_count, sources) / panels
    second = first - jnp.einsum("kmj,mj->kj", gram, first, precision=highest)
    total = first + second
    twice = image - jnp.einsum("kj,knjc->njc", total, basis, precision=highest)
    square = all_sum(jnp.sum(twice * twice, axis=(0, 2))) / panels
    beta = jnp.sqrt(square + 1e-06)
    next_vector = twice / beta[None, :, None]
    hess_column = jnp.concatenate([total, beta[None, :]], axis=0)
    return (next_vector, hess_column)


def solution(mesh):
    in_specs = (
        P(None, AXES, None, None),
        P(AXES, None),
        P(AXES, None, None),
        P(AXES, None, None),
        P(AXES, None, None),
        P(AXES),
        P(AXES, None),
        P(AXES),
    )
    out_specs = (P(AXES, None, None), P())
    return jax.shard_map(
        on_device, mesh=mesh, in_specs=in_specs, out_specs=out_specs, check_vma=False
    )
```

```python
import jax
import jax.numpy as jnp
from jax import lax
from jax.experimental import pallas as pl
from jax.experimental.pallas import tpu as pltpu
from jax.sharding import PartitionSpec as P


AXES = ("grp", "dev")
SIZES = {"y": 4, "z": 4, "x": 4, "c": 2}
STRIDE = {"y": 32, "z": 8, "x": 2, "c": 1}


def coord(g, axis):
    return (g // STRIDE[axis]) % SIZES[axis]


def moved(axis, k, other=None):
    pairs = []
    for g in range(128):
        a = other if (other is not None and g % 2 == 1) else axis
        n, s = SIZES[a], STRIDE[a]
        c = (g // s) % n
        pairs.append((g, g + (((c + k) % n) - c) * s))
    return pairs


def flipped(mask):
    return [(g, g ^ mask) for g in range(128)]


def all_sum(v):
    v = v + lax.ppermute(v, AXES, flipped(1))
    for axis in ("x", "z", "y"):
        for step in (1, 3):
            v = v + lax.ppermute(v, AXES, flipped(step * STRIDE[axis]))
    return v


def spread(pieces, axis, other=None):
    acc = pieces[0]
    for k in (1, 2, 3):
        acc = acc + lax.ppermute(pieces[k], AXES, moved(axis, k, other))
    return acc


def reduce_to_owner(keep, send):
    pieces = [keep[k] + lax.ppermute(send[k], AXES, moved("c", 1)) for k in range(4)]
    acc = pieces[0]
    for k in (1, 2, 3):
        acc = acc + lax.ppermute(pieces[k], AXES, moved("x", k, "z"))
    d = spread(acc, "z", "x")
    return d, spread(d, "y")


STEPS = 8


def accumulate_kernel(slot_ref, near_ref, far_ref, keep_ref, send_ref):
    i = pl.program_id(0)
    half = keep_ref.shape[0]
    near_step = near_ref.shape[0]
    far_step = far_ref.shape[0]
    near_total = near_step * pl.num_programs(0)

    @pl.when(i == 0)
    def _():
        keep_ref[...] = jnp.zeros_like(keep_ref)
        send_ref[...] = jnp.zeros_like(send_ref)

    def add(g, part):
        s = slot_ref[g]

        @pl.when(s < half)
        def _():
            keep_ref[s] += part

        @pl.when(s >= half)
        def _():
            send_ref[s - half] += part

    for j in range(near_step):
        add(i * near_step + j, near_ref[j])
    for j in range(far_step):
        add(near_total + i * far_step + j, far_ref[j])


def accumulate(slot, near_part, far_part, half):
    near_count, sources, size = near_part.shape
    far_count = far_part.shape[0]
    near_step = near_count // STEPS
    far_step = far_count // STEPS
    out = jax.ShapeDtypeStruct((half, sources, size), jnp.float32)
    grid_spec = pltpu.PrefetchScalarGridSpec(
        num_scalar_prefetch=1,
        grid=(STEPS,),
        in_specs=[
            pl.BlockSpec((near_step, sources, size), lambda i, s: (i, 0, 0)),
            pl.BlockSpec((far_step, sources, size), lambda i, s: (i, 0, 0)),
        ],
        out_specs=[
            pl.BlockSpec((half, sources, size), lambda i, s: (0, 0, 0)),
            pl.BlockSpec((half, sources, size), lambda i, s: (0, 0, 0)),
        ],
    )
    return pl.pallas_call(
        accumulate_kernel,
        grid_spec=grid_spec,
        out_shape=[out, out],
        compiler_params=pltpu.CompilerParams(
            dimension_semantics=("arbitrary",), vmem_limit_bytes=48 * 1024 * 1024
        ),
    )(slot, near_part, far_part)


def step(basis, diagonal, near_blocks, far_u, far_v, block_row, block_dest, block_col):
    highest = lax.Precision.HIGHEST
    basis_count = basis.shape[0]
    clusters = basis.shape[1]
    sources = basis.shape[2]
    cluster_size = basis.shape[3]
    near_count = near_blocks.shape[0]
    devices = lax.axis_size(AXES)
    me = lax.axis_index(AXES)
    vector = basis[basis_count - 1]
    vec_low = vector.astype(jnp.bfloat16)
    picked = vec_low[block_row]
    near_part = jnp.einsum(
        "snc,scd->snd", picked[:near_count], near_blocks, preferred_element_type=jnp.float32
    )
    coeff = jnp.einsum(
        "snc,skc->snk", picked[near_count:], far_u, preferred_element_type=jnp.float32
    ).astype(jnp.bfloat16)
    far_part = jnp.einsum("snk,skc->snc", coeff, far_v, preferred_element_type=jnp.float32)
    dest = block_dest[:, 0]
    rel = {a: (coord(dest, a) - coord(me, a)) % SIZES[a] for a in SIZES}
    to_core = coord(dest, "c")
    order = jnp.where(to_core == 0, rel["x"] * 4 + rel["z"], rel["z"] * 4 + rel["x"])
    slot = ((rel["c"] * 16 + order) * 4 + rel["y"]) * clusters + block_col
    spots = devices * clusters
    keep, send = accumulate(slot, near_part, far_part, spots // 2)
    shape = (4, 4, 4, clusters, sources, cluster_size)
    peer_basis = [lax.ppermute(basis, AXES, moved("y", -k)) for k in (1, 2, 3)]
    partial, summed = reduce_to_owner(keep.reshape(shape), send.reshape(shape))
    own = diagonal[:, None, :] * vector
    image = own + summed
    panels = clusters * cluster_size * devices
    local_first = jnp.einsum("knjc,njc->kj", basis, own + partial[0], precision=highest)
    for k in (1, 2, 3):
        local_first = local_first + jnp.einsum(
            "knjc,njc->kj", peer_basis[k - 1], partial[k], precision=highest
        )
    local_gram = jnp.einsum("knjc,mnjc->kmj", basis, basis, precision=highest)
    both = all_sum(jnp.concatenate([local_first, local_gram.reshape(-1, sources)], axis=0))
    first = both[:basis_count] / panels
    gram = both[basis_count:].reshape(basis_count, basis_count, sources) / panels
    second = first - jnp.einsum("kmj,mj->kj", gram, first, precision=highest)
    total = first + second
    twice = image - jnp.einsum("kj,knjc->njc", total, basis, precision=highest)
    square = all_sum(jnp.sum(twice * twice, axis=(0, 2))) / panels
    beta = jnp.sqrt(square + 1e-06)
    next_vector = twice / beta[None, :, None]
    hess_column = jnp.concatenate([total, beta[None, :]], axis=0)
    return (next_vector, hess_column)


def solution(mesh):
    in_specs = (
        P(None, AXES, None, None),
        P(AXES, None),
        P(AXES, None, None),
        P(AXES, None, None),
        P(AXES, None, None),
        P(AXES),
        P(AXES, None),
        P(AXES),
    )
    out_specs = (P(AXES, None, None), P())
    return jax.shard_map(step, mesh=mesh, in_specs=in_specs, out_specs=out_specs, check_vma=False)
```

```python
import jax
import jax.numpy as jnp
from jax import lax
from jax.experimental import pallas as pl
from jax.experimental.pallas import tpu as pltpu
from jax.sharding import PartitionSpec as P

AXES = ("grp", "dev")
SIZES = {"y": 4, "z": 4, "x": 4, "c": 2}
STRIDE = {"y": 32, "z": 8, "x": 2, "c": 1}


def coord(g, axis):
    return (g // STRIDE[axis]) % SIZES[axis]


def moved(axis, k, other=None):
    pairs = []
    for g in range(128):
        a = other if (other is not None and g % 2 == 1) else axis
        n, s = SIZES[a], STRIDE[a]
        c = (g // s) % n
        pairs.append((g, g + (((c + k) % n) - c) * s))
    return pairs


def flipped(mask):
    return [(g, g ^ mask) for g in range(128)]


def all_sum(v):
    v = v + lax.ppermute(v, AXES, flipped(1))
    for axis in ("x", "z", "y"):
        for step in (1, 3):
            v = v + lax.ppermute(v, AXES, flipped(step * STRIDE[axis]))
    return v


def spread(pieces, axis, other=None):
    acc = pieces[0]
    for k in (1, 2, 3):
        acc = acc + lax.ppermute(pieces[k], AXES, moved(axis, k, other))
    return acc


def reduce_to_owner(keep, send):
    pieces = [keep[k] + lax.ppermute(send[k], AXES, moved("c", 1)) for k in range(4)]
    acc = pieces[0]
    for k in (1, 2, 3):
        acc = acc + lax.ppermute(pieces[k], AXES, moved("x", k, "z"))
    d = spread(acc, "z", "x")
    return spread(d, "y")


STEPS = 8


def accumulate_kernel(slot_ref, near_ref, far_ref, keep_ref, send_ref):
    i = pl.program_id(0)
    half = keep_ref.shape[0]
    near_step = near_ref.shape[0]
    far_step = far_ref.shape[0]
    near_total = near_step * pl.num_programs(0)

    @pl.when(i == 0)
    def _():
        keep_ref[...] = jnp.zeros_like(keep_ref)
        send_ref[...] = jnp.zeros_like(send_ref)

    def add(g, part):
        s = slot_ref[g]

        @pl.when(s < half)
        def _():
            keep_ref[s] += part

        @pl.when(s >= half)
        def _():
            send_ref[s - half] += part

    for j in range(near_step):
        add(i * near_step + j, near_ref[j])
    for j in range(far_step):
        add(near_total + i * far_step + j, far_ref[j])


def accumulate(slot, near_part, far_part, half):
    near_count, sources, size = near_part.shape
    far_count = far_part.shape[0]
    near_step = near_count // STEPS
    far_step = far_count // STEPS
    out = jax.ShapeDtypeStruct((half, sources, size), jnp.float32)
    grid_spec = pltpu.PrefetchScalarGridSpec(
        num_scalar_prefetch=1,
        grid=(STEPS,),
        in_specs=[
            pl.BlockSpec((near_step, sources, size), lambda i, s: (i, 0, 0)),
            pl.BlockSpec((far_step, sources, size), lambda i, s: (i, 0, 0)),
        ],
        out_specs=[
            pl.BlockSpec((half, sources, size), lambda i, s: (0, 0, 0)),
            pl.BlockSpec((half, sources, size), lambda i, s: (0, 0, 0)),
        ],
    )
    return pl.pallas_call(
        accumulate_kernel,
        grid_spec=grid_spec,
        out_shape=[out, out],
        compiler_params=pltpu.CompilerParams(
            dimension_semantics=("arbitrary",), vmem_limit_bytes=48 * 1024 * 1024
        ),
    )(slot, near_part, far_part)


def on_device(basis, diagonal, near_blocks, far_u, far_v, block_row, block_dest, block_col):
    highest = lax.Precision.HIGHEST
    basis_count = basis.shape[0]
    clusters = basis.shape[1]
    sources = basis.shape[2]
    cluster_size = basis.shape[3]
    near_count = near_blocks.shape[0]
    devices = lax.axis_size(AXES)
    me = lax.axis_index(AXES)
    vector = basis[basis_count - 1]
    vec_low = vector.astype(jnp.bfloat16)
    picked = vec_low[block_row]
    near_part = jnp.einsum(
        "snc,scd->snd", picked[:near_count], near_blocks, preferred_element_type=jnp.float32
    )
    coeff = jnp.einsum(
        "snc,skc->snk", picked[near_count:], far_u, preferred_element_type=jnp.float32
    ).astype(jnp.bfloat16)
    far_part = jnp.einsum("snk,skc->snc", coeff, far_v, preferred_element_type=jnp.float32)
    dest = block_dest[:, 0]
    rel = {a: (coord(dest, a) - coord(me, a)) % SIZES[a] for a in SIZES}
    to_core = coord(dest, "c")
    order = jnp.where(to_core == 0, rel["x"] * 4 + rel["z"], rel["z"] * 4 + rel["x"])
    slot = ((rel["c"] * 16 + order) * 4 + rel["y"]) * clusters + block_col
    spots = devices * clusters
    keep, send = accumulate(slot, near_part, far_part, spots // 2)
    shape = (4, 4, 4, clusters, sources, cluster_size)
    summed = reduce_to_owner(keep.reshape(shape), send.reshape(shape))
    image = diagonal[:, None, :] * vector + summed
    panels = clusters * cluster_size * devices
    local_first = jnp.einsum("knjc,njc->kj", basis, image, precision=highest)
    local_gram = jnp.einsum("knjc,mnjc->kmj", basis, basis, precision=highest)
    local_size = jnp.sum(image * image, axis=(0, 2))[None, :]
    both = all_sum(
        jnp.concatenate([local_first, local_gram.reshape(-1, sources), local_size], axis=0)
    )
    first = both[:basis_count] / panels
    gram = both[basis_count:-1].reshape(basis_count, basis_count, sources) / panels
    size = both[-1] / panels
    second = first - jnp.einsum("kmj,mj->kj", gram, first, precision=highest)
    total = first + second
    twice = image - jnp.einsum("kj,knjc->njc", total, basis, precision=highest)
    cross = jnp.sum(total * first, axis=0)
    curve = jnp.sum(total * jnp.einsum("kmj,mj->kj", gram, total, precision=highest), axis=0)
    formula = size - 2.0 * cross + curve
    trusted = jnp.all(formula >= 0.01 * (size + 2.0 * jnp.abs(cross) + jnp.abs(curve)))
    square = lax.cond(
        trusted,
        lambda: formula,
        lambda: all_sum(jnp.sum(twice * twice, axis=(0, 2))) / panels,
    )
    beta = jnp.sqrt(square + 1e-06)
    next_vector = twice / beta[None, :, None]
    hess_column = jnp.concatenate([total, beta[None, :]], axis=0)
    return (next_vector, hess_column)


def solution(mesh):
    in_specs = (
        P(None, AXES, None, None),
        P(AXES, None),
        P(AXES, None, None),
        P(AXES, None, None),
        P(AXES, None, None),
        P(AXES),
        P(AXES, None),
        P(AXES),
    )
    out_specs = (P(AXES, None, None), P())
    return jax.shard_map(
        on_device, mesh=mesh, in_specs=in_specs, out_specs=out_specs, check_vma=False
    )
```

```python
import jax
import jax.numpy as jnp
from jax import lax
from jax.experimental import pallas as pl
from jax.experimental.pallas import tpu as pltpu
from jax.sharding import PartitionSpec as P

AXES = ("grp", "dev")
SIZES = {"y": 4, "z": 4, "x": 4, "c": 2}
STRIDE = {"y": 32, "z": 8, "x": 2, "c": 1}


def coord(g, axis):
    return (g // STRIDE[axis]) % SIZES[axis]


def moved(axis, k, other=None):
    pairs = []
    for g in range(128):
        a = other if (other is not None and g % 2 == 1) else axis
        n, s = SIZES[a], STRIDE[a]
        c = (g // s) % n
        pairs.append((g, g + (((c + k) % n) - c) * s))
    return pairs


def flipped(mask):
    return [(g, g ^ mask) for g in range(128)]


def all_sum(v):
    v = v + lax.ppermute(v, AXES, flipped(1))
    for axis in ("x", "z", "y"):
        for step in (1, 3):
            v = v + lax.ppermute(v, AXES, flipped(step * STRIDE[axis]))
    return v


def spread(pieces, axis, other=None):
    acc = pieces[0]
    for k in (1, 2, 3):
        acc = acc + lax.ppermute(pieces[k], AXES, moved(axis, k, other))
    return acc


def reduce_to_owner(keep, send):
    pieces = [keep[k] + lax.ppermute(send[k], AXES, moved("c", 1)) for k in range(4)]
    acc = pieces[0]
    for k in (1, 2, 3):
        acc = acc + lax.ppermute(pieces[k], AXES, moved("x", k, "z"))
    d = spread(acc, "z", "x")
    return spread(d, "y")


STEPS = 8


def accumulate_kernel(slot_ref, near_ref, far_ref, *refs):
    *out_refs, total_ref = refs
    i = pl.program_id(0)
    piece = out_refs[0].shape[0]
    near_step = near_ref.shape[0]
    far_step = far_ref.shape[0]
    near_total = near_step * pl.num_programs(0)

    @pl.when(i == 0)
    def _():
        total_ref[...] = jnp.zeros_like(total_ref)

    for j in range(near_step):
        total_ref[slot_ref[i * near_step + j]] += near_ref[j]
    for j in range(far_step):
        total_ref[slot_ref[near_total + i * far_step + j]] += far_ref[j]

    @pl.when(i == pl.num_programs(0) - 1)
    def _():
        for number, ref in enumerate(out_refs):
            ref[...] = total_ref[number * piece:(number + 1) * piece]


def accumulate(slot, near_part, far_part, spots, pieces):
    near_count, sources, size = near_part.shape
    far_count = far_part.shape[0]
    near_step = near_count // STEPS
    far_step = far_count // STEPS
    length = spots // pieces
    out = jax.ShapeDtypeStruct((length, sources, size), jnp.float32)
    grid_spec = pltpu.PrefetchScalarGridSpec(
        num_scalar_prefetch=1,
        grid=(STEPS,),
        in_specs=[
            pl.BlockSpec((near_step, sources, size), lambda i, s: (i, 0, 0)),
            pl.BlockSpec((far_step, sources, size), lambda i, s: (i, 0, 0)),
        ],
        out_specs=[pl.BlockSpec((length, sources, size), lambda i, s: (0, 0, 0))] * pieces,
        scratch_shapes=[pltpu.VMEM((spots, sources, size), jnp.float32)],
    )
    return pl.pallas_call(
        accumulate_kernel,
        grid_spec=grid_spec,
        out_shape=[out] * pieces,
        compiler_params=pltpu.CompilerParams(
            dimension_semantics=("arbitrary",), vmem_limit_bytes=48 * 1024 * 1024
        ),
    )(slot, near_part, far_part)


def on_device(basis, diagonal, near_blocks, far_u, far_v, block_row, block_dest, block_col):
    highest = lax.Precision.HIGHEST
    basis_count = basis.shape[0]
    clusters = basis.shape[1]
    sources = basis.shape[2]
    cluster_size = basis.shape[3]
    near_count = near_blocks.shape[0]
    devices = lax.axis_size(AXES)
    me = lax.axis_index(AXES)
    vector = basis[basis_count - 1]
    vec_low = vector.astype(jnp.bfloat16)
    picked = vec_low[block_row]
    near_part = jnp.einsum(
        "snc,scd->snd", picked[:near_count], near_blocks, preferred_element_type=jnp.float32
    )
    coeff = jnp.einsum(
        "snc,skc->snk", picked[near_count:], far_u, preferred_element_type=jnp.float32
    ).astype(jnp.bfloat16)
    far_part = jnp.einsum("snk,skc->snc", coeff, far_v, preferred_element_type=jnp.float32)
    dest = block_dest[:, 0]
    rel = {a: (coord(dest, a) - coord(me, a)) % SIZES[a] for a in SIZES}
    to_core = coord(dest, "c")
    order = jnp.where(to_core == 0, rel["x"] * 4 + rel["z"], rel["z"] * 4 + rel["x"])
    slot = ((rel["c"] * 16 + order) * 4 + rel["y"]) * clusters + block_col
    spots = devices * clusters
    parts = accumulate(slot, near_part, far_part, spots, 8)
    shape = (4, 4, clusters, sources, cluster_size)
    parts = [p.reshape(shape) for p in parts]
    summed = reduce_to_owner(parts[:4], parts[4:])
    image = diagonal[:, None, :] * vector + summed
    panels = clusters * cluster_size * devices
    local_first = jnp.einsum("knjc,njc->kj", basis, image, precision=highest)
    local_gram = jnp.einsum("knjc,mnjc->kmj", basis, basis, precision=highest)
    local_size = jnp.sum(image * image, axis=(0, 2))[None, :]
    both = all_sum(
        jnp.concatenate([local_first, local_gram.reshape(-1, sources), local_size], axis=0)
    )
    first = both[:basis_count] / panels
    gram = both[basis_count:-1].reshape(basis_count, basis_count, sources) / panels
    size = both[-1] / panels
    second = first - jnp.einsum("kmj,mj->kj", gram, first, precision=highest)
    total = first + second
    twice = image - jnp.einsum("kj,knjc->njc", total, basis, precision=highest)
    cross = jnp.sum(total * first, axis=0)
    curve = jnp.sum(total * jnp.einsum("kmj,mj->kj", gram, total, precision=highest), axis=0)
    formula = size - 2.0 * cross + curve
    trusted = jnp.all(formula >= 0.01 * (size + 2.0 * jnp.abs(cross) + jnp.abs(curve)))
    square = lax.cond(
        trusted,
        lambda: formula,
        lambda: all_sum(jnp.sum(twice * twice, axis=(0, 2))) / panels,
    )
    beta = jnp.sqrt(square + 1e-06)
    next_vector = twice / beta[None, :, None]
    hess_column = jnp.concatenate([total, beta[None, :]], axis=0)
    return (next_vector, hess_column)


def solution(mesh):
    in_specs = (
        P(None, AXES, None, None),
        P(AXES, None),
        P(AXES, None, None),
        P(AXES, None, None),
        P(AXES, None, None),
        P(AXES),
        P(AXES, None),
        P(AXES),
    )
    out_specs = (P(AXES, None, None), P())
    return jax.shard_map(
        on_device, mesh=mesh, in_specs=in_specs, out_specs=out_specs, check_vma=False
    )
```

```python
import jax
import jax.numpy as jnp
from jax import lax
from jax.experimental import pallas as pl
from jax.experimental.pallas import tpu as pltpu
from jax.sharding import PartitionSpec as P

AXES = ("grp", "dev")
SIZES = {"y": 4, "z": 4, "x": 4, "c": 2}
STRIDE = {"y": 32, "z": 8, "x": 2, "c": 1}


def coord(g, axis):
    return (g // STRIDE[axis]) % SIZES[axis]


def moved(axis, k, other=None):
    pairs = []
    for g in range(128):
        a = other if (other is not None and g % 2 == 1) else axis
        n, s = SIZES[a], STRIDE[a]
        c = (g // s) % n
        pairs.append((g, g + (((c + k) % n) - c) * s))
    return pairs


def flipped(mask):
    return [(g, g ^ mask) for g in range(128)]


def all_sum(v):
    v = v + lax.ppermute(v, AXES, flipped(1))
    for axis in ("x", "z", "y"):
        for step in (1, 3):
            v = v + lax.ppermute(v, AXES, flipped(step * STRIDE[axis]))
    return v


def spread(pieces, axis, other=None):
    acc = pieces[0]
    for k in (1, 2, 3):
        acc = acc + lax.ppermute(pieces[k], AXES, moved(axis, k, other))
    return acc


def reduce_to_owner(keep, send):
    pieces = [keep[k] + lax.ppermute(send[k], AXES, moved("c", 1)) for k in range(4)]
    acc = pieces[0]
    for k in (1, 2, 3):
        acc = acc + lax.ppermute(pieces[k], AXES, moved("x", k, "z"))
    d = spread(acc, "z", "x")
    return spread(d, "y")


STEPS = 8


def accumulate_kernel(slot_ref, near_ref, far_ref, *refs):
    *out_refs, total_ref = refs
    i = pl.program_id(0)
    piece = out_refs[0].shape[0]
    near_step = near_ref.shape[0]
    far_step = far_ref.shape[0]
    near_total = near_step * pl.num_programs(0)

    @pl.when(i == 0)
    def _():
        total_ref[...] = jnp.zeros_like(total_ref)

    for j in range(near_step):
        total_ref[slot_ref[i * near_step + j]] += near_ref[j]
    for j in range(far_step):
        total_ref[slot_ref[near_total + i * far_step + j]] += far_ref[j]

    @pl.when(i == pl.num_programs(0) - 1)
    def _():
        for number, ref in enumerate(out_refs):
            ref[...] = total_ref[number * piece:(number + 1) * piece]


def accumulate(slot, near_part, far_part, spots, pieces):
    near_count, sources, size = near_part.shape
    far_count = far_part.shape[0]
    near_step = near_count // STEPS
    far_step = far_count // STEPS
    length = spots // pieces
    out = jax.ShapeDtypeStruct((length, sources, size), jnp.float32)
    grid_spec = pltpu.PrefetchScalarGridSpec(
        num_scalar_prefetch=1,
        grid=(STEPS,),
        in_specs=[
            pl.BlockSpec((near_step, sources, size), lambda i, s: (i, 0, 0)),
            pl.BlockSpec((far_step, sources, size), lambda i, s: (i, 0, 0)),
        ],
        out_specs=[pl.BlockSpec((length, sources, size), lambda i, s: (0, 0, 0))] * pieces,
        scratch_shapes=[pltpu.VMEM((spots, sources, size), jnp.float32)],
    )
    return pl.pallas_call(
        accumulate_kernel,
        grid_spec=grid_spec,
        out_shape=[out] * pieces,
        compiler_params=pltpu.CompilerParams(
            dimension_semantics=("arbitrary",), vmem_limit_bytes=28 * 1024 * 1024
        ),
    )(slot, near_part, far_part)


def on_device(basis, diagonal, near_blocks, far_u, far_v, block_row, block_dest, block_col):
    highest = lax.Precision.HIGHEST
    basis_count = basis.shape[0]
    clusters = basis.shape[1]
    sources = basis.shape[2]
    cluster_size = basis.shape[3]
    near_count = near_blocks.shape[0]
    devices = lax.axis_size(AXES)
    me = lax.axis_index(AXES)
    vector = basis[basis_count - 1]
    vec_low = vector.astype(jnp.bfloat16)
    picked = vec_low[block_row]
    near_part = jnp.einsum(
        "snc,scd->snd", picked[:near_count], near_blocks, preferred_element_type=jnp.float32
    )
    coeff = jnp.einsum(
        "snc,skc->snk", picked[near_count:], far_u, preferred_element_type=jnp.float32
    ).astype(jnp.bfloat16)
    far_part = jnp.einsum("snk,skc->snc", coeff, far_v, preferred_element_type=jnp.float32)
    dest = block_dest[:, 0]
    rel = {a: (coord(dest, a) - coord(me, a)) % SIZES[a] for a in SIZES}
    to_core = coord(dest, "c")
    order = jnp.where(to_core == 0, rel["x"] * 4 + rel["z"], rel["z"] * 4 + rel["x"])
    slot = ((rel["c"] * 16 + order) * 4 + rel["y"]) * clusters + block_col
    spots = devices * clusters
    parts = accumulate(slot, near_part, far_part, spots, 8)
    shape = (4, 4, clusters, sources, cluster_size)
    parts = [p.reshape(shape) for p in parts]
    summed = reduce_to_owner(parts[:4], parts[4:])
    image = diagonal[:, None, :] * vector + summed
    panels = clusters * cluster_size * devices
    local_first = jnp.einsum("knjc,njc->kj", basis, image, precision=highest)
    local_gram = jnp.einsum("knjc,mnjc->kmj", basis, basis, precision=highest)
    local_size = jnp.sum(image * image, axis=(0, 2))[None, :]
    both = all_sum(
        jnp.concatenate([local_first, local_gram.reshape(-1, sources), local_size], axis=0)
    )
    first = both[:basis_count] / panels
    gram = both[basis_count:-1].reshape(basis_count, basis_count, sources) / panels
    size = both[-1] / panels
    second = first - jnp.einsum("kmj,mj->kj", gram, first, precision=highest)
    total = first + second
    twice = image - jnp.einsum("kj,knjc->njc", total, basis, precision=highest)
    cross = jnp.sum(total * first, axis=0)
    curve = jnp.sum(total * jnp.einsum("kmj,mj->kj", gram, total, precision=highest), axis=0)
    formula = size - 2.0 * cross + curve
    trusted = jnp.all(formula >= 0.01 * (size + 2.0 * jnp.abs(cross) + jnp.abs(curve)))
    square = lax.cond(
        trusted,
        lambda: formula,
        lambda: all_sum(jnp.sum(twice * twice, axis=(0, 2))) / panels,
    )
    beta = jnp.sqrt(square + 1e-06)
    next_vector = twice / beta[None, :, None]
    hess_column = jnp.concatenate([total, beta[None, :]], axis=0)
    return (next_vector, hess_column)


def solution(mesh):
    in_specs = (
        P(None, AXES, None, None),
        P(AXES, None),
        P(AXES, None, None),
        P(AXES, None, None),
        P(AXES, None, None),
        P(AXES),
        P(AXES, None),
        P(AXES),
    )
    out_specs = (P(AXES, None, None), P())
    return jax.shard_map(
        on_device, mesh=mesh, in_specs=in_specs, out_specs=out_specs, check_vma=False
    )
```

```python
import jax
import jax.numpy as jnp
from jax import lax
from jax.experimental import pallas as pl
from jax.experimental.pallas import tpu as pltpu
from jax.sharding import PartitionSpec as P

AXES = ("grp", "dev")
SIZES = {"y": 4, "z": 4, "x": 4, "c": 2}
STRIDE = {"y": 32, "z": 8, "x": 2, "c": 1}


def coord(g, axis):
    return (g // STRIDE[axis]) % SIZES[axis]


def moved(axis, k, other=None):
    pairs = []
    for g in range(128):
        a = other if (other is not None and g % 2 == 1) else axis
        n, s = SIZES[a], STRIDE[a]
        c = (g // s) % n
        pairs.append((g, g + (((c + k) % n) - c) * s))
    return pairs


def flipped(mask):
    return [(g, g ^ mask) for g in range(128)]


def all_sum(v):
    v = v + lax.ppermute(v, AXES, flipped(1))
    for axis in ("x", "z", "y"):
        for step in (1, 3):
            v = v + lax.ppermute(v, AXES, flipped(step * STRIDE[axis]))
    return v


def spread(pieces, axis, other=None):
    acc = pieces[0]
    for k in (1, 2, 3):
        acc = acc + lax.ppermute(pieces[k], AXES, moved(axis, k, other))
    return acc


def reduce_to_owner(keep, send):
    pieces = [keep[k] + lax.ppermute(send[k], AXES, moved("c", 1)) for k in range(4)]
    acc = pieces[0]
    for k in (1, 2, 3):
        acc = acc + lax.ppermute(pieces[k], AXES, moved("x", k, "z"))
    d = spread(acc, "z", "x")
    return spread(d, "y")


STEPS = 8


def accumulate_kernel(slot_ref, near_ref, far_ref, *refs):
    *out_refs, total_ref = refs
    i = pl.program_id(0)
    piece = out_refs[0].shape[0]
    near_step = near_ref.shape[0]
    far_step = far_ref.shape[0]
    near_total = near_step * pl.num_programs(0)

    @pl.when(i == 0)
    def _():
        total_ref[...] = jnp.zeros_like(total_ref)

    for j in range(near_step):
        total_ref[slot_ref[i * near_step + j]] += near_ref[j]
    for j in range(far_step):
        total_ref[slot_ref[near_total + i * far_step + j]] += far_ref[j]

    @pl.when(i == pl.num_programs(0) - 1)
    def _():
        for number, ref in enumerate(out_refs):
            ref[...] = total_ref[number * piece:(number + 1) * piece]


def accumulate(slot, near_part, far_part, spots, pieces):
    near_count, sources, size = near_part.shape
    far_count = far_part.shape[0]
    near_step = near_count // STEPS
    far_step = far_count // STEPS
    length = spots // pieces
    out = jax.ShapeDtypeStruct((length, sources, size), jnp.float32)
    grid_spec = pltpu.PrefetchScalarGridSpec(
        num_scalar_prefetch=1,
        grid=(STEPS,),
        in_specs=[
            pl.BlockSpec((near_step, sources, size), lambda i, s: (i, 0, 0)),
            pl.BlockSpec((far_step, sources, size), lambda i, s: (i, 0, 0)),
        ],
        out_specs=[pl.BlockSpec((length, sources, size), lambda i, s: (0, 0, 0))] * pieces,
        scratch_shapes=[pltpu.VMEM((spots, sources, size), jnp.float32)],
    )
    return pl.pallas_call(
        accumulate_kernel,
        grid_spec=grid_spec,
        out_shape=[out] * pieces,
        compiler_params=pltpu.CompilerParams(
            dimension_semantics=("arbitrary",), vmem_limit_bytes=28 * 1024 * 1024
        ),
    )(slot, near_part, far_part)


def on_device(basis, diagonal, near_blocks, far_u, far_v, block_row, block_dest, block_col):
    highest = lax.Precision.HIGHEST
    basis_count = basis.shape[0]
    clusters = basis.shape[1]
    sources = basis.shape[2]
    cluster_size = basis.shape[3]
    near_count = near_blocks.shape[0]
    devices = lax.axis_size(AXES)
    me = lax.axis_index(AXES)
    vector = basis[basis_count - 1]
    vec_low = vector.astype(jnp.bfloat16)
    picked = vec_low[block_row]
    near_part = jnp.einsum(
        "snc,scd->snd", picked[:near_count], near_blocks, preferred_element_type=jnp.float32
    )
    both_rows = jnp.einsum("rnc,skc->srnk", vec_low, far_u, preferred_element_type=jnp.float32)
    far_rows = block_row[near_count:]
    coeff = jnp.where(
        (far_rows == 0)[:, None, None], both_rows[:, 0], both_rows[:, 1]
    ).astype(jnp.bfloat16)
    far_part = jnp.einsum("snk,skc->snc", coeff, far_v, preferred_element_type=jnp.float32)
    dest = block_dest[:, 0]
    rel = {a: (coord(dest, a) - coord(me, a)) % SIZES[a] for a in SIZES}
    to_core = coord(dest, "c")
    order = jnp.where(to_core == 0, rel["x"] * 4 + rel["z"], rel["z"] * 4 + rel["x"])
    slot = ((rel["c"] * 16 + order) * 4 + rel["y"]) * clusters + block_col
    spots = devices * clusters
    parts = accumulate(slot, near_part, far_part, spots, 8)
    shape = (4, 4, clusters, sources, cluster_size)
    parts = [p.reshape(shape) for p in parts]
    summed = reduce_to_owner(parts[:4], parts[4:])
    image = diagonal[:, None, :] * vector + summed
    panels = clusters * cluster_size * devices
    local_first = jnp.einsum("knjc,njc->kj", basis, image, precision=highest)
    local_gram = jnp.einsum("knjc,mnjc->kmj", basis, basis, precision=highest)
    local_size = jnp.sum(image * image, axis=(0, 2))[None, :]
    both = all_sum(
        jnp.concatenate([local_first, local_gram.reshape(-1, sources), local_size], axis=0)
    )
    first = both[:basis_count] / panels
    gram = both[basis_count:-1].reshape(basis_count, basis_count, sources) / panels
    size = both[-1] / panels
    second = first - jnp.einsum("kmj,mj->kj", gram, first, precision=highest)
    total = first + second
    twice = image - jnp.einsum("kj,knjc->njc", total, basis, precision=highest)
    cross = jnp.sum(total * first, axis=0)
    curve = jnp.sum(total * jnp.einsum("kmj,mj->kj", gram, total, precision=highest), axis=0)
    formula = size - 2.0 * cross + curve
    trusted = jnp.all(formula >= 0.01 * (size + 2.0 * jnp.abs(cross) + jnp.abs(curve)))
    square = lax.cond(
        trusted,
        lambda: formula,
        lambda: all_sum(jnp.sum(twice * twice, axis=(0, 2))) / panels,
    )
    beta = jnp.sqrt(square + 1e-06)
    next_vector = twice / beta[None, :, None]
    hess_column = jnp.concatenate([total, beta[None, :]], axis=0)
    return (next_vector, hess_column)


def solution(mesh):
    in_specs = (
        P(None, AXES, None, None),
        P(AXES, None),
        P(AXES, None, None),
        P(AXES, None, None),
        P(AXES, None, None),
        P(AXES),
        P(AXES, None),
        P(AXES),
    )
    out_specs = (P(AXES, None, None), P())
    return jax.shard_map(
        on_device, mesh=mesh, in_specs=in_specs, out_specs=out_specs, check_vma=False
    )
```

```python
import jax
import jax.numpy as jnp
from jax import lax
from jax.experimental import pallas as pl
from jax.experimental.pallas import tpu as pltpu
from jax.sharding import PartitionSpec as P


AXES = ("grp", "dev")
SIZES = {"y": 4, "z": 4, "x": 4, "c": 2}
STRIDE = {"y": 32, "z": 8, "x": 2, "c": 1}


def coord(g, axis):
    return (g // STRIDE[axis]) % SIZES[axis]


def moved(axis, k, other=None):
    pairs = []
    for g in range(128):
        a = other if (other is not None and g % 2 == 1) else axis
        n, s = SIZES[a], STRIDE[a]
        c = (g // s) % n
        pairs.append((g, g + (((c + k) % n) - c) * s))
    return pairs


def flipped(mask):
    return [(g, g ^ mask) for g in range(128)]


def all_sum(v):
    v = v + lax.ppermute(v, AXES, flipped(1))
    for axis in ("x", "z", "y"):
        for step in (1, 3):
            v = v + lax.ppermute(v, AXES, flipped(step * STRIDE[axis]))
    return v


def spread(pieces, axis, other=None):
    acc = pieces[0]
    for k in (1, 2, 3):
        acc = acc + lax.ppermute(pieces[k], AXES, moved(axis, k, other))
    return acc


def reduce_to_owner(keep, send):
    pieces = [keep[k] + lax.ppermute(send[k], AXES, moved("c", 1)) for k in range(4)]
    far = lax.ppermute(pieces[2], AXES, moved("x", 2, "z"))
    near = [lax.ppermute(pieces[k], AXES, moved("x", k, "z")) for k in (1, 3)]
    acc = pieces[0] + near[0] + far + near[1]
    d = spread(acc, "z", "x")
    return spread(d, "y")


STEPS = 8


def accumulate_kernel(slot_ref, near_ref, far_ref, *refs):
    *out_refs, total_ref = refs
    i = pl.program_id(0)
    piece = out_refs[0].shape[0]
    near_step = near_ref.shape[0]
    far_step = far_ref.shape[0]
    near_total = near_step * pl.num_programs(0)

    @pl.when(i == 0)
    def _():
        total_ref[...] = jnp.zeros_like(total_ref)

    for j in range(near_step):
        total_ref[slot_ref[i * near_step + j]] += near_ref[j]
    for j in range(far_step):
        total_ref[slot_ref[near_total + i * far_step + j]] += far_ref[j]

    @pl.when(i == pl.num_programs(0) - 1)
    def _():
        for number, ref in enumerate(out_refs):
            ref[...] = total_ref[number * piece:(number + 1) * piece]


def accumulate(slot, near_part, far_part, spots, pieces):
    near_count, sources, size = near_part.shape
    far_count = far_part.shape[0]
    near_step = near_count // STEPS
    far_step = far_count // STEPS
    length = spots // pieces
    out = jax.ShapeDtypeStruct((length, sources, size), jnp.float32)
    grid_spec = pltpu.PrefetchScalarGridSpec(
        num_scalar_prefetch=1,
        grid=(STEPS,),
        in_specs=[
            pl.BlockSpec((near_step, sources, size), lambda i, s: (i, 0, 0)),
            pl.BlockSpec((far_step, sources, size), lambda i, s: (i, 0, 0)),
        ],
        out_specs=[pl.BlockSpec((length, sources, size), lambda i, s: (0, 0, 0))] * pieces,
        scratch_shapes=[pltpu.VMEM((spots, sources, size), jnp.float32)],
    )
    return pl.pallas_call(
        accumulate_kernel,
        grid_spec=grid_spec,
        out_shape=[out] * pieces,
        compiler_params=pltpu.CompilerParams(
            dimension_semantics=("arbitrary",), vmem_limit_bytes=28 * 1024 * 1024
        ),
    )(slot, near_part, far_part)


def step(basis, diagonal, near_blocks, far_u, far_v, block_row, block_dest, block_col):
    highest = lax.Precision.HIGHEST
    basis_count = basis.shape[0]
    clusters = basis.shape[1]
    sources = basis.shape[2]
    cluster_size = basis.shape[3]
    near_count = near_blocks.shape[0]
    devices = lax.axis_size(AXES)
    me = lax.axis_index(AXES)
    vector = basis[basis_count - 1]
    vec_low = vector.astype(jnp.bfloat16)
    picked = vec_low[block_row]
    near_part = jnp.einsum(
        "snc,scd->snd", picked[:near_count], near_blocks, preferred_element_type=jnp.float32
    )
    coeff = jnp.einsum(
        "snc,skc->snk", picked[near_count:], far_u, preferred_element_type=jnp.float32
    ).astype(jnp.bfloat16)
    far_part = jnp.einsum("snk,skc->snc", coeff, far_v, preferred_element_type=jnp.float32)
    dest = block_dest[:, 0]
    rel = {a: (coord(dest, a) - coord(me, a)) % SIZES[a] for a in SIZES}
    to_core = coord(dest, "c")
    order = jnp.where(to_core == 0, rel["x"] * 4 + rel["z"], rel["z"] * 4 + rel["x"])
    slot = ((rel["c"] * 16 + order) * 4 + rel["y"]) * clusters + block_col
    spots = devices * clusters
    parts = accumulate(slot, near_part, far_part, spots, 8)
    shape = (4, 4, clusters, sources, cluster_size)
    parts = [p.reshape(shape) for p in parts]
    summed = reduce_to_owner(parts[:4], parts[4:])
    image = diagonal[:, None, :] * vector + summed
    panels = clusters * cluster_size * devices
    local_first = jnp.einsum("knjc,njc->kj", basis, image, precision=highest)
    local_gram = jnp.einsum("knjc,mnjc->kmj", basis, basis, precision=highest)
    local_size = jnp.sum(image * image, axis=(0, 2))[None, :]
    both = all_sum(
        jnp.concatenate([local_first, local_gram.reshape(-1, sources), local_size], axis=0)
    )
    first = both[:basis_count] / panels
    gram = both[basis_count:-1].reshape(basis_count, basis_count, sources) / panels
    size = both[-1] / panels
    second = first - jnp.einsum("kmj,mj->kj", gram, first, precision=highest)
    total = first + second
    twice = image - jnp.einsum("kj,knjc->njc", total, basis, precision=highest)
    cross = jnp.sum(total * first, axis=0)
    curve = jnp.sum(total * jnp.einsum("kmj,mj->kj", gram, total, precision=highest), axis=0)
    formula = size - 2.0 * cross + curve
    trusted = jnp.all(formula >= 0.01 * (size + 2.0 * jnp.abs(cross) + jnp.abs(curve)))
    square = lax.cond(
        trusted,
        lambda: formula,
        lambda: all_sum(jnp.sum(twice * twice, axis=(0, 2))) / panels,
    )
    beta = jnp.sqrt(square + 1e-06)
    next_vector = twice / beta[None, :, None]
    hess_column = jnp.concatenate([total, beta[None, :]], axis=0)
    return (next_vector, hess_column)


def solution(mesh):
    in_specs = (
        P(None, AXES, None, None),
        P(AXES, None),
        P(AXES, None, None),
        P(AXES, None, None),
        P(AXES, None, None),
        P(AXES),
        P(AXES, None),
        P(AXES),
    )
    out_specs = (P(AXES, None, None), P())
    return jax.shard_map(step, mesh=mesh, in_specs=in_specs, out_specs=out_specs, check_vma=False)
```

```python
import jax
import jax.numpy as jnp
from jax import lax
from jax.experimental import pallas as pl
from jax.experimental.pallas import tpu as pltpu
from jax.sharding import PartitionSpec as P


AXES = ("grp", "dev")
SIZES = {"y": 4, "z": 4, "x": 4, "c": 2}
STRIDE = {"y": 32, "z": 8, "x": 2, "c": 1}


def coord(g, axis):
    return (g // STRIDE[axis]) % SIZES[axis]


def moved(axis, k, other=None):
    pairs = []
    for g in range(128):
        a = other if (other is not None and g % 2 == 1) else axis
        n, s = SIZES[a], STRIDE[a]
        c = (g // s) % n
        pairs.append((g, g + (((c + k) % n) - c) * s))
    return pairs


def flipped(mask):
    return [(g, g ^ mask) for g in range(128)]


def all_sum(v):
    v = v + lax.ppermute(v, AXES, flipped(1))
    for axis in ("x", "z", "y"):
        for step in (1, 3):
            v = v + lax.ppermute(v, AXES, flipped(step * STRIDE[axis]))
    return v


def spread(pieces, axis, other=None):
    far = lax.ppermute(pieces[2], AXES, moved(axis, 2, other))
    near = [lax.ppermute(pieces[k], AXES, moved(axis, k, other)) for k in (1, 3)]
    return pieces[0] + near[0] + far + near[1]


def reduce_to_owner(keep, send):
    pieces = [keep[k] + lax.ppermute(send[k], AXES, moved("c", 1)) for k in range(4)]
    far = lax.ppermute(pieces[2], AXES, moved("x", 2, "z"))
    near = [lax.ppermute(pieces[k], AXES, moved("x", k, "z")) for k in (1, 3)]
    acc = pieces[0] + near[0] + far + near[1]
    d = spread(acc, "z", "x")
    return spread(d, "y")


STEPS = 8


def accumulate_kernel(slot_ref, near_ref, far_ref, *refs):
    *out_refs, total_ref = refs
    i = pl.program_id(0)
    piece = out_refs[0].shape[0]
    near_step = near_ref.shape[0]
    far_step = far_ref.shape[0]
    near_total = near_step * pl.num_programs(0)

    @pl.when(i == 0)
    def _():
        total_ref[...] = jnp.zeros_like(total_ref)

    for j in range(near_step):
        total_ref[slot_ref[i * near_step + j]] += near_ref[j]
    for j in range(far_step):
        total_ref[slot_ref[near_total + i * far_step + j]] += far_ref[j]

    @pl.when(i == pl.num_programs(0) - 1)
    def _():
        for number, ref in enumerate(out_refs):
            ref[...] = total_ref[number * piece:(number + 1) * piece]


def accumulate(slot, near_part, far_part, spots, pieces):
    near_count, sources, size = near_part.shape
    far_count = far_part.shape[0]
    near_step = near_count // STEPS
    far_step = far_count // STEPS
    length = spots // pieces
    out = jax.ShapeDtypeStruct((length, sources, size), jnp.float32)
    grid_spec = pltpu.PrefetchScalarGridSpec(
        num_scalar_prefetch=1,
        grid=(STEPS,),
        in_specs=[
            pl.BlockSpec((near_step, sources, size), lambda i, s: (i, 0, 0)),
            pl.BlockSpec((far_step, sources, size), lambda i, s: (i, 0, 0)),
        ],
        out_specs=[pl.BlockSpec((length, sources, size), lambda i, s: (0, 0, 0))] * pieces,
        scratch_shapes=[pltpu.VMEM((spots, sources, size), jnp.float32)],
    )
    return pl.pallas_call(
        accumulate_kernel,
        grid_spec=grid_spec,
        out_shape=[out] * pieces,
        compiler_params=pltpu.CompilerParams(
            dimension_semantics=("arbitrary",), vmem_limit_bytes=28 * 1024 * 1024
        ),
    )(slot, near_part, far_part)


def step(basis, diagonal, near_blocks, far_u, far_v, block_row, block_dest, block_col):
    highest = lax.Precision.HIGHEST
    basis_count = basis.shape[0]
    clusters = basis.shape[1]
    sources = basis.shape[2]
    cluster_size = basis.shape[3]
    near_count = near_blocks.shape[0]
    devices = lax.axis_size(AXES)
    me = lax.axis_index(AXES)
    vector = basis[basis_count - 1]
    vec_low = vector.astype(jnp.bfloat16)
    picked = vec_low[block_row]
    near_part = jnp.einsum(
        "snc,scd->snd", picked[:near_count], near_blocks, preferred_element_type=jnp.float32
    )
    coeff = jnp.einsum(
        "snc,skc->snk", picked[near_count:], far_u, preferred_element_type=jnp.float32
    ).astype(jnp.bfloat16)
    far_part = jnp.einsum("snk,skc->snc", coeff, far_v, preferred_element_type=jnp.float32)
    dest = block_dest[:, 0]
    rel = {a: (coord(dest, a) - coord(me, a)) % SIZES[a] for a in SIZES}
    to_core = coord(dest, "c")
    order = jnp.where(to_core == 0, rel["x"] * 4 + rel["z"], rel["z"] * 4 + rel["x"])
    slot = ((rel["c"] * 16 + order) * 4 + rel["y"]) * clusters + block_col
    spots = devices * clusters
    parts = accumulate(slot, near_part, far_part, spots, 8)
    shape = (4, 4, clusters, sources, cluster_size)
    parts = [p.reshape(shape) for p in parts]
    summed = reduce_to_owner(parts[:4], parts[4:])
    image = diagonal[:, None, :] * vector + summed
    panels = clusters * cluster_size * devices
    local_first = jnp.einsum("knjc,njc->kj", basis, image, precision=highest)
    local_gram = jnp.einsum("knjc,mnjc->kmj", basis, basis, precision=highest)
    local_size = jnp.sum(image * image, axis=(0, 2))[None, :]
    both = all_sum(
        jnp.concatenate([local_first, local_gram.reshape(-1, sources), local_size], axis=0)
    )
    first = both[:basis_count] / panels
    gram = both[basis_count:-1].reshape(basis_count, basis_count, sources) / panels
    size = both[-1] / panels
    second = first - jnp.einsum("kmj,mj->kj", gram, first, precision=highest)
    total = first + second
    twice = image - jnp.einsum("kj,knjc->njc", total, basis, precision=highest)
    cross = jnp.sum(total * first, axis=0)
    curve = jnp.sum(total * jnp.einsum("kmj,mj->kj", gram, total, precision=highest), axis=0)
    formula = size - 2.0 * cross + curve
    trusted = jnp.all(formula >= 0.01 * (size + 2.0 * jnp.abs(cross) + jnp.abs(curve)))
    square = lax.cond(
        trusted,
        lambda: formula,
        lambda: all_sum(jnp.sum(twice * twice, axis=(0, 2))) / panels,
    )
    beta = jnp.sqrt(square + 1e-06)
    next_vector = twice / beta[None, :, None]
    hess_column = jnp.concatenate([total, beta[None, :]], axis=0)
    return (next_vector, hess_column)


def solution(mesh):
    in_specs = (
        P(None, AXES, None, None),
        P(AXES, None),
        P(AXES, None, None),
        P(AXES, None, None),
        P(AXES, None, None),
        P(AXES),
        P(AXES, None),
        P(AXES),
    )
    out_specs = (P(AXES, None, None), P())
    return jax.shard_map(step, mesh=mesh, in_specs=in_specs, out_specs=out_specs, check_vma=False)
```

```python
import jax
import jax.numpy as jnp
from jax import lax
from jax.experimental import pallas as pl
from jax.experimental.pallas import tpu as pltpu
from jax.sharding import PartitionSpec as P


AXES = ("grp", "dev")
SIZES = {"y": 4, "z": 4, "x": 4, "c": 2}
STRIDE = {"y": 32, "z": 8, "x": 2, "c": 1}


def coord(g, axis):
    return (g // STRIDE[axis]) % SIZES[axis]


def moved(axis, k, other=None):
    pairs = []
    for g in range(128):
        a = other if (other is not None and g % 2 == 1) else axis
        n, s = SIZES[a], STRIDE[a]
        c = (g // s) % n
        pairs.append((g, g + (((c + k) % n) - c) * s))
    return pairs


def flipped(mask):
    return [(g, g ^ mask) for g in range(128)]


def all_sum(v):
    v = v + lax.ppermute(v, AXES, flipped(1))
    for axis in ("y", "z", "x"):
        for step in (1, 3):
            v = v + lax.ppermute(v, AXES, flipped(step * STRIDE[axis]))
    return v


def spread(pieces, axis, other=None):
    far = lax.ppermute(pieces[2], AXES, moved(axis, 2, other))
    near = [lax.ppermute(pieces[k], AXES, moved(axis, k, other)) for k in (1, 3)]
    return pieces[0] + near[0] + far + near[1]


def reduce_to_owner(keep, send):
    pieces = [keep[k] + lax.ppermute(send[k], AXES, moved("c", 1)) for k in range(4)]
    far = lax.ppermute(pieces[2], AXES, moved("x", 2, "z"))
    near = [lax.ppermute(pieces[k], AXES, moved("x", k, "z")) for k in (1, 3)]
    acc = pieces[0] + near[0] + far + near[1]
    d = spread(acc, "z", "x")
    return spread(d, "y")


STEPS = 8


def accumulate_kernel(slot_ref, near_ref, far_ref, *refs):
    *out_refs, total_ref = refs
    i = pl.program_id(0)
    piece = out_refs[0].shape[0]
    near_step = near_ref.shape[0]
    far_step = far_ref.shape[0]
    near_total = near_step * pl.num_programs(0)

    @pl.when(i == 0)
    def _():
        total_ref[...] = jnp.zeros_like(total_ref)

    for j in range(near_step):
        total_ref[slot_ref[i * near_step + j]] += near_ref[j]
    for j in range(far_step):
        total_ref[slot_ref[near_total + i * far_step + j]] += far_ref[j]

    @pl.when(i == pl.num_programs(0) - 1)
    def _():
        for number, ref in enumerate(out_refs):
            ref[...] = total_ref[number * piece:(number + 1) * piece]


def accumulate(slot, near_part, far_part, spots, pieces):
    near_count, sources, size = near_part.shape
    far_count = far_part.shape[0]
    near_step = near_count // STEPS
    far_step = far_count // STEPS
    length = spots // pieces
    out = jax.ShapeDtypeStruct((length, sources, size), jnp.float32)
    grid_spec = pltpu.PrefetchScalarGridSpec(
        num_scalar_prefetch=1,
        grid=(STEPS,),
        in_specs=[
            pl.BlockSpec((near_step, sources, size), lambda i, s: (i, 0, 0)),
            pl.BlockSpec((far_step, sources, size), lambda i, s: (i, 0, 0)),
        ],
        out_specs=[pl.BlockSpec((length, sources, size), lambda i, s: (0, 0, 0))] * pieces,
        scratch_shapes=[pltpu.VMEM((spots, sources, size), jnp.float32)],
    )
    return pl.pallas_call(
        accumulate_kernel,
        grid_spec=grid_spec,
        out_shape=[out] * pieces,
        compiler_params=pltpu.CompilerParams(
            dimension_semantics=("arbitrary",), vmem_limit_bytes=28 * 1024 * 1024
        ),
    )(slot, near_part, far_part)


def orthogonal(image, total, basis):
    return image - jnp.einsum("kj,knjc->njc", total, basis, precision=lax.Precision.HIGHEST)


def step(basis, diagonal, near_blocks, far_u, far_v, block_row, block_dest, block_col):
    highest = lax.Precision.HIGHEST
    basis_count = basis.shape[0]
    clusters = basis.shape[1]
    sources = basis.shape[2]
    cluster_size = basis.shape[3]
    near_count = near_blocks.shape[0]
    devices = lax.axis_size(AXES)
    me = lax.axis_index(AXES)
    vector = basis[basis_count - 1]
    vec_low = vector.astype(jnp.bfloat16)
    picked = vec_low[block_row]
    near_part = jnp.einsum(
        "snc,scd->snd", picked[:near_count], near_blocks, preferred_element_type=jnp.float32
    )
    coeff = jnp.einsum(
        "snc,skc->snk", picked[near_count:], far_u, preferred_element_type=jnp.float32
    ).astype(jnp.bfloat16)
    far_part = jnp.einsum("snk,skc->snc", coeff, far_v, preferred_element_type=jnp.float32)
    dest = block_dest[:, 0]
    rel = {a: (coord(dest, a) - coord(me, a)) % SIZES[a] for a in SIZES}
    to_core = coord(dest, "c")
    order = jnp.where(to_core == 0, rel["x"] * 4 + rel["z"], rel["z"] * 4 + rel["x"])
    slot = ((rel["c"] * 16 + order) * 4 + rel["y"]) * clusters + block_col
    spots = devices * clusters
    parts = accumulate(slot, near_part, far_part, spots, 8)
    shape = (4, 4, clusters, sources, cluster_size)
    parts = [p.reshape(shape) for p in parts]
    summed = reduce_to_owner(parts[:4], parts[4:])
    image = diagonal[:, None, :] * vector + summed
    panels = clusters * cluster_size * devices
    local_first = jnp.einsum("knjc,njc->kj", basis, image, precision=highest)
    local_gram = jnp.einsum("knjc,mnjc->kmj", basis, basis, precision=highest)
    local_size = jnp.sum(image * image, axis=(0, 2))[None, :]
    both = all_sum(
        jnp.concatenate([local_first, local_gram.reshape(-1, sources), local_size], axis=0)
    )
    first = both[:basis_count] / panels
    gram = both[basis_count:-1].reshape(basis_count, basis_count, sources) / panels
    size = both[-1] / panels
    second = first - jnp.einsum("kmj,mj->kj", gram, first, precision=highest)
    total = first + second
    cross = jnp.sum(total * first, axis=0)
    curve = jnp.sum(total * jnp.einsum("kmj,mj->kj", gram, total, precision=highest), axis=0)
    formula = size - 2.0 * cross + curve
    trusted = jnp.all(formula >= 0.01 * (size + 2.0 * jnp.abs(cross) + jnp.abs(curve)))
    square = lax.cond(
        trusted,
        lambda: formula,
        lambda: all_sum(jnp.sum(orthogonal(image, total, basis) ** 2, axis=(0, 2))) / panels,
    )
    twice = orthogonal(image, total, basis)
    beta = jnp.sqrt(square + 1e-06)
    next_vector = twice / beta[None, :, None]
    hess_column = jnp.concatenate([total, beta[None, :]], axis=0)
    return (next_vector, hess_column)


def solution(mesh):
    in_specs = (
        P(None, AXES, None, None),
        P(AXES, None),
        P(AXES, None, None),
        P(AXES, None, None),
        P(AXES, None, None),
        P(AXES),
        P(AXES, None),
        P(AXES),
    )
    out_specs = (P(AXES, None, None), P())
    return jax.shard_map(step, mesh=mesh, in_specs=in_specs, out_specs=out_specs, check_vma=False)
```
